128 devices in a mesh: row: 4 (over z_lo, core), col: 4 (over x), slab: 8 (over y, z_hi).
Axes of the slice: x: 4, y: 4, z: 4 (z_hi: 2, z_lo: 2; z = z_hi * 2 + z_lo), core: 2. Of those that a mesh axis runs over, the one named last changes fastest.
Arguments:
- amplitudes: bfloat16 [48, 48, 480, 128], P('row', 'col', 'slab'), may hold values from -6 to 6
- integrals: bfloat16 [48, 480, 48, 128], P('row', 'slab', 'col'), may hold values from -0.0625 to 0.0625
- irreps: int32 [19], replicated, may hold values from 0 to 1
- pair_mask: int32 [4, 4], replicated, may hold values 0 or 1
Outputs:
- cycle_term: bfloat16 [48, 48, 128, 128], P('row', 'col', 'slab')
The draws below stay inside these ranges and needn't reach their ends.
Inputs may be any that keep to these rules, and one draw needn't show every extreme that they name: Each label is one of the two irreps of the point group. `pair_mask`: 1 marks a block pair whose amplitudes are kept.
All inputs are finite; a program needn't handle non-finite values.
Results may differ from the reference program's by a relative error of at most 0.001.
Values may be sent and summed in bfloat16 or wider, within the bound.
No kernel may reach another device: no remote copies, remote signals or barrier semaphores. Data moves between devices by JAX's collectives and lax.ppermute only.
A program may use at most 128 MiB of HBM per device.

```python
import jax
import jax.numpy as jnp

O = 48
V = 480
OBLK = 12
VTILE = 32
NBO = 4
NTV = 15
WIN = 128


def place_ends(entries, rng, least, largest):
    extent = entries.shape
    place = [jax.random.randint(jax.random.fold_in(rng, axis), (), 0, extent[axis]) for axis in range(len(extent))]
    entries = entries.at[tuple(place)].set(least)
    longest = extent.index(max(extent))
    place[longest] = (place[longest] + 1) % extent[longest]
    return entries.at[tuple(place)].set(largest)


def shard_levels(own_key, dims, split, smallest, largest):
    loudness = 1.0
    for dim, blocks in split:
        draws = jax.random.uniform(jax.random.fold_in(jax.random.fold_in(own_key, 6), dim), (blocks,), jnp.float32, smallest / len(split), largest / len(split))
        loudness = loudness * jnp.repeat(jnp.exp(draws), dims[dim] // blocks).reshape((-1,) + (1,) * (len(dims) - 1 - dim))
    return loudness


def gaussian(own_key, shape, scale, bound, shards=(), kind=jnp.bfloat16):
    factor_of = shard_levels(own_key, shape, shards, -0.22, 0.18) if shards else 1.0
    entries = jax.random.normal(own_key, shape, jnp.float32) * scale * factor_of
    return jnp.minimum(jnp.maximum(entries, -bound), bound).astype(kind)


def setup_inputs(seed: int = 0) -> dict:
    keys = jax.random.split(jax.random.key(seed), 5)
    amplitudes = gaussian(keys[0], (O, O, V, WIN), 1.0, 6.0, ((0, 4), (1, 4), (2, 8)))
    integrals = gaussian(keys[1], (O, V, O, WIN), (O * V // 3) ** -0.5, 0.0625, ((0, 4), (1, 8), (2, 4)))
    irreps = place_ends(jax.random.randint(keys[2], (NBO + NTV,), 0, 2), jax.random.fold_in(keys[2], 1), 0, 1).astype(jnp.int32)
    pair_mask = place_ends((jax.random.randint(keys[3], (NBO, NBO), 0, 4) < 3).astype(jnp.int32), jax.random.fold_in(keys[3], 1), 0, 1)
    return dict(amplitudes=amplitudes, integrals=integrals, irreps=irreps, pair_mask=pair_mask)


def reference(amplitudes, integrals, irreps, pair_mask):
    blocks = O // OBLK
    occ_block = jnp.arange(O, dtype=jnp.int32) // OBLK
    vir_tile = jnp.arange(V, dtype=jnp.int32) // VTILE
    pair_factor = pair_mask[occ_block][:, occ_block].astype(jnp.float32)
    amp_masked = amplitudes.astype(jnp.float32) * pair_factor[:, :, None, None]
    occ_label = irreps[occ_block]
    vir_label = irreps[blocks + vir_tile]
    win_label = vir_label[:WIN]
    parity = occ_label[:, None, None, None] + vir_label[None, :, None, None] + occ_label[None, None, :, None] + win_label[None, None, None, :]
    int_masked = jnp.where(parity % 2 == 0, integrals.astype(jnp.float32), jnp.zeros((), jnp.float32))
    cycle = jnp.einsum("ikca,kcjb->ijab", amp_masked, int_masked)
    return (cycle + jnp.transpose(cycle, (1, 0, 3, 2))).astype(jnp.bfloat16)
```

```python
import jax
import jax.numpy as jnp
from jax import lax
from jax.sharding import PartitionSpec as P

OBLK = 12
VTILE = 32


def shifted(value, axis, fn):
    size = lax.axis_size(axis)
    return lax.ppermute(value, axis, [(src, fn(src) % size) for src in range(size)])


def int_mask(irreps, blocks, row_at, col_at, slab_at, c_cols, win_cols):
    c_ids = slab_at * c_cols + jnp.arange(c_cols, dtype=jnp.int32)
    b_ids = jnp.arange(win_cols, dtype=jnp.int32)
    label_c = jnp.take(irreps, blocks + c_ids // VTILE)
    label_b = jnp.take(irreps, blocks + b_ids // VTILE)
    occ = irreps[row_at] + irreps[col_at]
    parity = occ + label_c[:, None] + label_b[None, :]
    return parity % 2 == 0


def gather_col(amp):
    near1 = shifted(amp, "col", lambda c: c ^ 1)
    near3 = shifted(amp, "col", lambda c: c ^ 3)
    half = amp.shape[0] // 2
    far_a = shifted(near3[:half], "col", lambda c: c ^ 1)
    far_b = shifted(near1[half:], "col", lambda c: c ^ 3)
    far = jnp.concatenate([far_a, far_b], axis=0)
    return [amp, near1, far, near3]


def gather_row(ints):
    zpart = shifted(ints, "row", lambda r: r ^ 2)
    pair = jnp.stack([ints, zpart])
    other = shifted(pair, "row", lambda r: r ^ 1)
    return jnp.stack([ints, other[0], zpart, other[1]])


def ring_reduce_y(part, slab_at):
    ny = lax.axis_size("slab") // 2
    width = part.shape[2] // ny
    y_at = slab_at // 2
    half = part.shape[0] // 2
    halves = (part[:half], part[half:])
    dirs = (1, -1)
    acc = [None, None]
    for step in range(ny - 1):
        for h in range(2):
            d = dirs[h]
            chunk = (y_at - d * (step + 1)) % ny
            own = lax.dynamic_slice_in_dim(halves[h], chunk * width, width, axis=2)
            send = own if acc[h] is None else acc[h] + own
            acc[h] = shifted(send, "slab", lambda s, d=d: s + 2 * d)
    result = []
    for h in range(2):
        own = lax.dynamic_slice_in_dim(halves[h], y_at * width, width, axis=2)
        result.append(acc[h] + own)
    return jnp.concatenate(result, axis=0)


def body(amplitudes, integrals, irreps, pair_mask):
    i_rows, k_rows, c_cols, win_cols = amplitudes.shape
    blocks = pair_mask.shape[0]
    row_at = lax.axis_index("row")
    col_at = lax.axis_index("col")
    slab_at = lax.axis_index("slab")
    n_slab = lax.axis_size("slab")

    keep = pair_mask[row_at, col_at] != 0
    amp = jnp.where(keep, amplitudes, jnp.zeros_like(amplitudes))
    mask = int_mask(irreps, blocks, row_at, col_at, slab_at, c_cols, win_cols)
    ints = jnp.where(mask[None, :, None, :], integrals, jnp.zeros_like(integrals))

    amp_x = gather_col(amp)
    int_x = gather_row(ints)
    part = None
    for v in range(4):
        u = (col_at ^ v) ^ row_at
        int_blk = lax.dynamic_index_in_dim(int_x, u, axis=0, keepdims=False)
        term = jnp.einsum("ikca,kcjb->ijab", amp_x[v], int_blk, preferred_element_type=jnp.float32)
        part = term if part is None else part + term

    reduced_y = ring_reduce_y(part, slab_at)
    zh = slab_at % 2
    width = reduced_y.shape[2] // 2
    mine = lax.dynamic_slice_in_dim(reduced_y, zh * width, width, axis=2)
    theirs = lax.dynamic_slice_in_dim(reduced_y, (1 - zh) * width, width, axis=2)
    shares = mine + shifted(theirs, "slab", lambda s: s ^ 1)

    n_row = lax.axis_size("row")
    n_col = lax.axis_size("col")
    axes = ("row", "col", "slab")
    tiles = []
    for d in range(n_slab):
        dest_slab = slab_at ^ d
        tile = lax.dynamic_slice_in_dim(shares, dest_slab * width, width, axis=3)
        pairs = []
        for r in range(n_row):
            for c in range(n_col):
                for t in range(n_slab):
                    pairs.append(((r * n_col + c) * n_slab + t, (c * n_col + r) * n_slab + (t ^ d)))
        tiles.append(lax.ppermute(tile, axes, pairs))
    stacked = jnp.stack(tiles)
    order = jnp.arange(n_slab, dtype=jnp.int32) ^ slab_at
    ordered = jnp.take(stacked, order, axis=0)
    mirrored = jnp.transpose(ordered, (2, 1, 4, 0, 3)).reshape(shares.shape)
    return (shares + mirrored).astype(jnp.bfloat16)


def solution(mesh):
    return jax.shard_map(
        body,
        mesh=mesh,
        in_specs=(P("row", "col", "slab", None), P("row", "slab", "col", None), P(), P()),
        out_specs=P("row", "col", "slab", None),
        check_vma=False,
    )
```

```python
import jax
import jax.numpy as jnp
from jax import lax
from jax.sharding import PartitionSpec as P

OBLK = 12
VTILE = 32


def shifted(value, axis, fn):
    size = lax.axis_size(axis)
    return lax.ppermute(value, axis, [(src, fn(src) % size) for src in range(size)])


def int_mask(irreps, blocks, row_at, col_at, slab_at, c_cols, win_cols):
    c_ids = slab_at * c_cols + jnp.arange(c_cols, dtype=jnp.int32)
    b_ids = jnp.arange(win_cols, dtype=jnp.int32)
    label_c = jnp.take(irreps, blocks + c_ids // VTILE)
    label_b = jnp.take(irreps, blocks + b_ids // VTILE)
    occ = irreps[row_at] + irreps[col_at]
    parity = occ + label_c[:, None] + label_b[None, :]
    return parity % 2 == 0


def gather_col(amp):
    near1 = shifted(amp, "col", lambda c: c ^ 1)
    near3 = shifted(amp, "col", lambda c: c ^ 3)
    half = amp.shape[0] // 2
    far_a = shifted(near3[:half], "col", lambda c: c ^ 1)
    far_b = shifted(near1[half:], "col", lambda c: c ^ 3)
    far = jnp.concatenate([far_a, far_b], axis=0)
    return [amp, near1, far, near3]


def gather_row(ints):
    zpart = shifted(ints, "row", lambda r: r ^ 2)
    pair = jnp.stack([ints, zpart])
    other = shifted(pair, "row", lambda r: r ^ 1)
    return jnp.stack([ints, other[0], zpart, other[1]])


def ring_reduce_y(part, slab_at):
    ny = lax.axis_size("slab") // 2
    width = part.shape[2] // ny
    y_at = slab_at // 2
    half = part.shape[0] // 2
    halves = (part[:half], part[half:])
    dirs = (1, -1)
    acc = [None, None]
    for step in range(ny - 1):
        for h in range(2):
            d = dirs[h]
            chunk = (y_at - d * (step + 1)) % ny
            own = lax.dynamic_slice_in_dim(halves[h], chunk * width, width, axis=2)
            send = own if acc[h] is None else acc[h] + own
            acc[h] = shifted(send, "slab", lambda s, d=d: s + 2 * d)
    result = []
    for h in range(2):
        own = lax.dynamic_slice_in_dim(halves[h], y_at * width, width, axis=2)
        result.append(acc[h] + own)
    return jnp.concatenate(result, axis=0)


def body(amplitudes, integrals, irreps, pair_mask):
    i_rows, k_rows, c_cols, win_cols = amplitudes.shape
    blocks = pair_mask.shape[0]
    row_at = lax.axis_index("row")
    col_at = lax.axis_index("col")
    slab_at = lax.axis_index("slab")
    n_slab = lax.axis_size("slab")

    keep = pair_mask[row_at, col_at] != 0
    amp = jnp.where(keep, amplitudes, jnp.zeros_like(amplitudes))
    mask = int_mask(irreps, blocks, row_at, col_at, slab_at, c_cols, win_cols)
    ints = jnp.where(mask[None, :, None, :], integrals, jnp.zeros_like(integrals))

    amp_x = gather_col(amp)
    int_x = gather_row(ints)
    amp_x, int_x = lax.optimization_barrier((amp_x, int_x))
    part = None
    for v in range(4):
        u = (col_at ^ v) ^ row_at
        int_blk = lax.dynamic_index_in_dim(int_x, u, axis=0, keepdims=False)
        term = jnp.einsum("ikca,kcjb->ijab", amp_x[v], int_blk, preferred_element_type=jnp.float32)
        part = term if part is None else part + term

    reduced_y = ring_reduce_y(part, slab_at)
    zh = slab_at % 2
    width = reduced_y.shape[2] // 2
    mine = lax.dynamic_slice_in_dim(reduced_y, zh * width, width, axis=2)
    theirs = lax.dynamic_slice_in_dim(reduced_y, (1 - zh) * width, width, axis=2)
    shares = mine + shifted(theirs, "slab", lambda s: s ^ 1)

    n_row = lax.axis_size("row")
    n_col = lax.axis_size("col")
    i_n, j_n, a_n, b_n = shares.shape
    tiles = jnp.transpose(shares.reshape(i_n, j_n, a_n, n_slab, b_n // n_slab), (3, 0, 1, 2, 4))
    regrouped = lax.all_to_all(tiles, "slab", 0, 0, tiled=True)
    pairs = [(r * n_col + c, c * n_col + r) for r in range(n_row) for c in range(n_col)]
    swapped = lax.ppermute(regrouped, ("row", "col"), pairs)
    mirrored = jnp.transpose(swapped, (2, 1, 4, 0, 3)).reshape(shares.shape)
    return (shares + mirrored).astype(jnp.bfloat16)


def solution(mesh):
    return jax.shard_map(
        body,
        mesh=mesh,
        in_specs=(P("row", "col", "slab", None), P("row", "slab", "col", None), P(), P()),
        out_specs=P("row", "col", "slab", None),
        check_vma=False,
    )
```

```python
import jax
import jax.numpy as jnp
from jax import lax
from jax.sharding import PartitionSpec as P

OBLK = 12
VTILE = 32


def shifted(value, axis, fn):
    size = lax.axis_size(axis)
    return lax.ppermute(value, axis, [(src, fn(src) % size) for src in range(size)])


def int_mask(irreps, blocks, row_at, col_at, slab_at, c_cols, win_cols):
    c_ids = slab_at * c_cols + jnp.arange(c_cols, dtype=jnp.int32)
    b_ids = jnp.arange(win_cols, dtype=jnp.int32)
    label_c = jnp.take(irreps, blocks + c_ids // VTILE)
    label_b = jnp.take(irreps, blocks + b_ids // VTILE)
    occ = irreps[row_at] + irreps[col_at]
    parity = occ + label_c[:, None] + label_b[None, :]
    return parity % 2 == 0


def gather_row(ints):
    zpart = shifted(ints, "row", lambda r: r ^ 2)
    pair = jnp.stack([ints, zpart])
    other = shifted(pair, "row", lambda r: r ^ 1)
    return jnp.stack([ints, other[0], zpart, other[1]])


def ring_reduce_y(part, slab_at):
    ny = lax.axis_size("slab") // 2
    width = part.shape[2] // ny
    y_at = slab_at // 2
    half = part.shape[0] // 2
    halves = (part[:half], part[half:])
    dirs = (1, -1)
    acc = [None, None]
    for step in range(ny - 1):
        for h in range(2):
            d = dirs[h]
            chunk = (y_at - d * (step + 1)) % ny
            own = lax.dynamic_slice_in_dim(halves[h], chunk * width, width, axis=2)
            send = own if acc[h] is None else acc[h] + own
            acc[h] = shifted(send, "slab", lambda s, d=d: s + 2 * d)
    result = []
    for h in range(2):
        own = lax.dynamic_slice_in_dim(halves[h], y_at * width, width, axis=2)
        result.append(acc[h] + own)
    return jnp.concatenate(result, axis=0)


def body(amplitudes, integrals, irreps, pair_mask):
    i_rows, k_rows, c_cols, win_cols = amplitudes.shape
    blocks = pair_mask.shape[0]
    row_at = lax.axis_index("row")
    col_at = lax.axis_index("col")
    slab_at = lax.axis_index("slab")
    n_slab = lax.axis_size("slab")

    keep = pair_mask[row_at, col_at] != 0
    amp = jnp.where(keep, amplitudes, jnp.zeros_like(amplitudes))
    mask = int_mask(irreps, blocks, row_at, col_at, slab_at, c_cols, win_cols)
    ints = jnp.where(mask[None, :, None, :], integrals, jnp.zeros_like(integrals))

    amp_all = lax.all_gather(amp, "col", axis=1, tiled=True)
    int_x = gather_row(ints)
    order = jnp.arange(int_x.shape[0], dtype=jnp.int32) ^ row_at
    int_abs = jnp.take(int_x, order, axis=0).reshape(amp_all.shape[1], c_cols, -1, win_cols)
    part = jnp.einsum("ikca,kcjb->ijab", amp_all, int_abs, preferred_element_type=jnp.float32)

    reduced_y = ring_reduce_y(part, slab_at)
    zh = slab_at % 2
    width = reduced_y.shape[2] // 2
    mine = lax.dynamic_slice_in_dim(reduced_y, zh * width, width, axis=2)
    theirs = lax.dynamic_slice_in_dim(reduced_y, (1 - zh) * width, width, axis=2)
    shares = mine + shifted(theirs, "slab", lambda s: s ^ 1)

    spread = lax.all_to_all(shares, "slab", 3, 2, tiled=True)
    mirrored = jnp.transpose(spread, (1, 0, 3, 2))
    for bit_no in range(lax.axis_size("row").bit_length() - 1):
        across = shifted(shifted(mirrored, "row", lambda r: r ^ 2**bit_no), "col", lambda c: c ^ 2**bit_no)
        differ = row_at // 2**bit_no % 2 != col_at // 2**bit_no % 2
        mirrored = jnp.where(differ, across, mirrored)
    return (shares + mirrored).astype(jnp.bfloat16)


def solution(mesh):
    return jax.shard_map(
        body,
        mesh=mesh,
        in_specs=(P("row", "col", "slab", None), P("row", "slab", "col", None), P(), P()),
        out_specs=P("row", "col", "slab", None),
        check_vma=False,
    )
```

```python
import jax
import jax.numpy as jnp
from jax import lax
from jax.sharding import PartitionSpec as P

OBLK = 12
VTILE = 32


def shifted(value, axis, fn):
    size = lax.axis_size(axis)
    return lax.ppermute(value, axis, [(src, fn(src) % size) for src in range(size)])


def int_mask(irreps, blocks, row_at, col_at, slab_at, c_cols, win_cols):
    c_ids = slab_at * c_cols + jnp.arange(c_cols, dtype=jnp.int32)
    b_ids = jnp.arange(win_cols, dtype=jnp.int32)
    label_c = jnp.take(irreps, blocks + c_ids // VTILE)
    label_b = jnp.take(irreps, blocks + b_ids // VTILE)
    occ = irreps[row_at] + irreps[col_at]
    parity = occ + label_c[:, None] + label_b[None, :]
    return parity % 2 == 0


def gather_row(ints, row_at):
    zpart = shifted(ints, "row", lambda r: r ^ 2)
    blocks = [ints, shifted(ints, "row", lambda r: r ^ 1), zpart, shifted(zpart, "row", lambda r: r ^ 1)]
    k_rows = ints.shape[0]
    whole = jnp.zeros((len(blocks) * k_rows,) + ints.shape[1:], ints.dtype)
    for u, blk in enumerate(blocks):
        whole = lax.dynamic_update_slice_in_dim(whole, blk, (row_at ^ u) * k_rows, axis=0)
    return whole


def ring_reduce_y(part, slab_at):
    ny = lax.axis_size("slab") // 2
    width = part.shape[2] // ny
    y_at = slab_at // 2
    half = part.shape[0] // 2
    halves = (part[:half], part[half:])
    dirs = (1, -1)
    acc = [None, None]
    for step in range(ny - 1):
        for h in range(2):
            d = dirs[h]
            chunk = (y_at - d * (step + 1)) % ny
            own = lax.dynamic_slice_in_dim(halves[h], chunk * width, width, axis=2)
            send = own if acc[h] is None else acc[h] + own
            acc[h] = shifted(send, "slab", lambda s, d=d: s + 2 * d)
    result = []
    for h in range(2):
        own = lax.dynamic_slice_in_dim(halves[h], y_at * width, width, axis=2)
        result.append(acc[h] + own)
    return jnp.concatenate(result, axis=0)


def body(amplitudes, integrals, irreps, pair_mask):
    i_rows, k_rows, c_cols, win_cols = amplitudes.shape
    blocks = pair_mask.shape[0]
    row_at = lax.axis_index("row")
    col_at = lax.axis_index("col")
    slab_at = lax.axis_index("slab")
    n_slab = lax.axis_size("slab")

    keep = pair_mask[row_at, col_at] != 0
    amp = jnp.where(keep, amplitudes, jnp.zeros_like(amplitudes))
    mask = int_mask(irreps, blocks, row_at, col_at, slab_at, c_cols, win_cols)
    ints = jnp.where(mask[None, :, None, :], integrals, jnp.zeros_like(integrals))

    amp_all = lax.all_gather(amp, "col", axis=1, tiled=True)
    int_abs = gather_row(ints, row_at)
    part = jnp.einsum("ikca,kcjb->ijab", amp_all, int_abs, preferred_element_type=jnp.float32)

    reduced_y = ring_reduce_y(part, slab_at)
    zh = slab_at % 2
    width = reduced_y.shape[2] // 2
    mine = lax.dynamic_slice_in_dim(reduced_y, zh * width, width, axis=2)
    theirs = lax.dynamic_slice_in_dim(reduced_y, (1 - zh) * width, width, axis=2)
    shares = mine + shifted(theirs, "slab", lambda s: s ^ 1)

    i_n, j_n, a_n, b_n = shares.shape
    mirrored = jnp.zeros((j_n, i_n, a_n, b_n), shares.dtype)
    for d in range(n_slab):
        tile = lax.dynamic_slice_in_dim(shares, (slab_at ^ d) * a_n, a_n, axis=3)
        tile = jnp.transpose(tile, (1, 0, 3, 2))
        if d:
            flat = shifted(tile.reshape(j_n * i_n, a_n * a_n), "slab", lambda t, d=d: t ^ d)
            tile = flat.reshape(j_n, i_n, a_n, a_n)
        mirrored = lax.dynamic_update_slice_in_dim(mirrored, tile, (slab_at ^ d) * a_n, axis=3)
    for bit_no in range(lax.axis_size("row").bit_length() - 1):
        across = shifted(shifted(mirrored, "row", lambda r: r ^ 2**bit_no), "col", lambda c: c ^ 2**bit_no)
        differ = row_at // 2**bit_no % 2 != col_at // 2**bit_no % 2
        mirrored = jnp.where(differ, across, mirrored)
    return (shares + mirrored).astype(jnp.bfloat16)


def solution(mesh):
    return jax.shard_map(
        body,
        mesh=mesh,
        in_specs=(P("row", "col", "slab", None), P("row", "slab", "col", None), P(), P()),
        out_specs=P("row", "col", "slab", None),
        check_vma=False,
    )
```

```python
import jax
import jax.numpy as jnp
from jax import lax
from jax.sharding import PartitionSpec as P

OBLK = 12
VTILE = 32


def shifted(value, axis, fn):
    size = lax.axis_size(axis)
    return lax.ppermute(value, axis, [(src, fn(src) % size) for src in range(size)])


def int_mask(irreps, blocks, row_at, col_at, slab_at, c_cols, win_cols):
    c_ids = slab_at * c_cols + jnp.arange(c_cols, dtype=jnp.int32)
    b_ids = jnp.arange(win_cols, dtype=jnp.int32)
    label_c = jnp.take(irreps, blocks + c_ids // VTILE)
    label_b = jnp.take(irreps, blocks + b_ids // VTILE)
    occ = irreps[row_at] + irreps[col_at]
    parity = occ + label_c[:, None] + label_b[None, :]
    return parity % 2 == 0


def gather_row(ints, row_at):
    zpart = shifted(ints, "row", lambda r: r ^ 2)
    blocks = [ints, shifted(ints, "row", lambda r: r ^ 1), zpart, shifted(zpart, "row", lambda r: r ^ 1)]
    k_rows = ints.shape[0]
    whole = jnp.zeros((len(blocks) * k_rows,) + ints.shape[1:], ints.dtype)
    for u, blk in enumerate(blocks):
        whole = lax.dynamic_update_slice_in_dim(whole, blk, (row_at ^ u) * k_rows, axis=0)
    return whole


def ring_reduce_y(part, slab_at):
    ny = lax.axis_size("slab") // 2
    width = part.shape[2] // ny
    y_at = slab_at // 2
    half = part.shape[0] // 2
    halves = (part[:half], part[half:])
    dirs = (1, -1)
    acc = [None, None]
    for step in range(ny - 1):
        for h in range(2):
            d = dirs[h]
            chunk = (y_at - d * (step + 1)) % ny
            own = lax.dynamic_slice_in_dim(halves[h], chunk * width, width, axis=2)
            send = own if acc[h] is None else acc[h] + own
            acc[h] = shifted(send, "slab", lambda s, d=d: s + 2 * d)
    result = []
    for h in range(2):
        own = lax.dynamic_slice_in_dim(halves[h], y_at * width, width, axis=2)
        result.append(acc[h] + own)
    return jnp.concatenate(result, axis=0)


def body(amplitudes, integrals, irreps, pair_mask):
    i_rows, k_rows, c_cols, win_cols = amplitudes.shape
    blocks = pair_mask.shape[0]
    row_at = lax.axis_index("row")
    col_at = lax.axis_index("col")
    slab_at = lax.axis_index("slab")
    n_slab = lax.axis_size("slab")

    keep = pair_mask[row_at, col_at] != 0
    amp = jnp.where(keep, amplitudes, jnp.zeros_like(amplitudes))
    mask = int_mask(irreps, blocks, row_at, col_at, slab_at, c_cols, win_cols)
    ints = jnp.where(mask[None, :, None, :], integrals, jnp.zeros_like(integrals))

    amp_all = lax.all_gather(amp, "col", axis=1, tiled=True)
    int_abs = gather_row(ints, row_at)
    part = jnp.einsum("ikca,kcjb->ijab", amp_all, int_abs, preferred_element_type=jnp.float32)

    reduced_y = ring_reduce_y(part, slab_at)
    zh = slab_at % 2
    width = reduced_y.shape[2] // 2
    mine = lax.dynamic_slice_in_dim(reduced_y, zh * width, width, axis=2)
    theirs = lax.dynamic_slice_in_dim(reduced_y, (1 - zh) * width, width, axis=2)
    shares = mine + shifted(theirs, "slab", lambda s: s ^ 1)

    i_n, j_n, a_n, b_n = shares.shape
    gathered = jnp.zeros((n_slab, j_n * i_n, a_n * a_n), shares.dtype)
    for d in range(n_slab):
        tile = lax.dynamic_slice_in_dim(shares, (slab_at ^ d) * a_n, a_n, axis=3)
        flat = jnp.transpose(tile, (1, 0, 3, 2)).reshape(1, j_n * i_n, a_n * a_n)
        if d:
            flat = shifted(flat, "slab", lambda t, d=d: t ^ d)
        gathered = lax.dynamic_update_slice_in_dim(gathered, flat, slab_at ^ d, axis=0)
    gathered = gathered.reshape(n_slab, j_n, i_n, a_n, a_n)
    mirrored = jnp.transpose(gathered, (1, 2, 3, 0, 4)).reshape(j_n, i_n, a_n, b_n)
    for bit_no in range(lax.axis_size("row").bit_length() - 1):
        across = shifted(shifted(mirrored, "row", lambda r: r ^ 2**bit_no), "col", lambda c: c ^ 2**bit_no)
        differ = row_at // 2**bit_no % 2 != col_at // 2**bit_no % 2
        mirrored = jnp.where(differ, across, mirrored)
    return (shares + mirrored).astype(jnp.bfloat16)


def solution(mesh):
    return jax.shard_map(
        body,
        mesh=mesh,
        in_specs=(P("row", "col", "slab", None), P("row", "slab", "col", None), P(), P()),
        out_specs=P("row", "col", "slab", None),
        check_vma=False,
    )
```

```python
import jax
import jax.numpy as jnp
from jax import lax
from jax.sharding import PartitionSpec as P

OBLK = 12
VTILE = 32


def shifted(value, axis, fn):
    size = lax.axis_size(axis)
    return lax.ppermute(value, axis, [(src, fn(src) % size) for src in range(size)])


def int_mask(irreps, blocks, row_at, col_at, slab_at, c_cols, win_cols):
    c_ids = slab_at * c_cols + jnp.arange(c_cols, dtype=jnp.int32)
    b_ids = jnp.arange(win_cols, dtype=jnp.int32)
    label_c = jnp.take(irreps, blocks + c_ids // VTILE)
    label_b = jnp.take(irreps, blocks + b_ids // VTILE)
    occ = irreps[row_at] + irreps[col_at]
    parity = occ + label_c[:, None] + label_b[None, :]
    return parity % 2 == 0


def gather_row(ints, row_at):
    zpart = shifted(ints, "row", lambda r: r ^ 2)
    blocks = [ints, shifted(ints, "row", lambda r: r ^ 1), zpart, shifted(zpart, "row", lambda r: r ^ 1)]
    k_rows = ints.shape[0]
    whole = jnp.zeros((len(blocks) * k_rows,) + ints.shape[1:], ints.dtype)
    for u, blk in enumerate(blocks):
        whole = lax.dynamic_update_slice_in_dim(whole, blk, (row_at ^ u) * k_rows, axis=0)
    return whole


def ring_reduce_y(part, slab_at):
    ny = lax.axis_size("slab") // 2
    width = part.shape[2] // ny
    y_at = slab_at // 2
    half = part.shape[0] // 2
    halves = (part[:half], part[half:])
    dirs = (1, -1)
    acc = [None, None]
    for step in range(ny - 1):
        for h in range(2):
            d = dirs[h]
            chunk = (y_at - d * (step + 1)) % ny
            own = lax.dynamic_slice_in_dim(halves[h], chunk * width, width, axis=2)
            send = own if acc[h] is None else acc[h] + own
            acc[h] = shifted(send, "slab", lambda s, d=d: s + 2 * d)
    result = []
    for h in range(2):
        own = lax.dynamic_slice_in_dim(halves[h], y_at * width, width, axis=2)
        result.append(acc[h] + own)
    return jnp.concatenate(result, axis=0)


def body(amplitudes, integrals, irreps, pair_mask):
    i_rows, k_rows, c_cols, win_cols = amplitudes.shape
    blocks = pair_mask.shape[0]
    row_at = lax.axis_index("row")
    col_at = lax.axis_index("col")
    slab_at = lax.axis_index("slab")
    n_slab = lax.axis_size("slab")

    keep = pair_mask[row_at, col_at] != 0
    amp = jnp.where(keep, amplitudes, jnp.zeros_like(amplitudes))
    mask = int_mask(irreps, blocks, row_at, col_at, slab_at, c_cols, win_cols)
    ints = jnp.where(mask[None, :, None, :], integrals, jnp.zeros_like(integrals))

    amp_all = lax.all_gather(amp, "col", axis=1, tiled=True)
    int_abs = gather_row(ints, row_at)
    part = jnp.einsum("ikca,kcjb->ijab", amp_all, int_abs, preferred_element_type=jnp.float32)

    reduced_y = ring_reduce_y(part, slab_at)
    zh = slab_at % 2
    width = reduced_y.shape[2] // 2
    mine = lax.dynamic_slice_in_dim(reduced_y, zh * width, width, axis=2)
    theirs = lax.dynamic_slice_in_dim(reduced_y, (1 - zh) * width, width, axis=2)
    shares = mine + shifted(theirs, "slab", lambda s: s ^ 1)

    n_row = lax.axis_size("row")
    n_col = lax.axis_size("col")
    i_n, j_n, a_n, b_n = shares.shape
    gathered = jnp.zeros((n_slab, j_n * i_n, a_n * a_n), shares.dtype)
    for d in range(n_slab):
        tile = lax.dynamic_slice_in_dim(shares, (slab_at ^ d) * a_n, a_n, axis=3)
        flat = jnp.transpose(tile, (1, 0, 3, 2)).reshape(1, j_n * i_n, a_n * a_n)
        pairs = [
            ((r * n_col + c) * n_slab + t, (c * n_col + r) * n_slab + (t ^ d))
            for r in range(n_row)
            for c in range(n_col)
            for t in range(n_slab)
        ]
        flat = lax.ppermute(flat, ("row", "col", "slab"), pairs)
        gathered = lax.dynamic_update_slice_in_dim(gathered, flat, slab_at ^ d, axis=0)
    gathered = gathered.reshape(n_slab, j_n, i_n, a_n, a_n)
    mirrored = jnp.transpose(gathered, (1, 2, 3, 0, 4)).reshape(shares.shape)
    return (shares + mirrored).astype(jnp.bfloat16)


def solution(mesh):
    return jax.shard_map(
        body,
        mesh=mesh,
        in_specs=(P("row", "col", "slab", None), P("row", "slab", "col", None), P(), P()),
        out_specs=P("row", "col", "slab", None),
        check_vma=False,
    )
```

```python
import jax
import jax.numpy as jnp
from jax import lax
from jax.sharding import PartitionSpec as P

OBLK = 12
VTILE = 32


def shifted(value, axis, fn):
    size = lax.axis_size(axis)
    return lax.ppermute(value, axis, [(src, fn(src) % size) for src in range(size)])


def int_mask(irreps, blocks, row_at, col_at, slab_at, c_cols, win_cols):
    c_ids = slab_at * c_cols + jnp.arange(c_cols, dtype=jnp.int32)
    b_ids = jnp.arange(win_cols, dtype=jnp.int32)
    label_c = jnp.take(irreps, blocks + c_ids // VTILE)
    label_b = jnp.take(irreps, blocks + b_ids // VTILE)
    occ = irreps[row_at] + irreps[col_at]
    parity = occ + label_c[:, None] + label_b[None, :]
    return parity % 2 == 0


def gather_row(ints, row_at):
    zpart = shifted(ints, "row", lambda r: r ^ 2)
    blocks = [ints, shifted(ints, "row", lambda r: r ^ 1), zpart, shifted(zpart, "row", lambda r: r ^ 1)]
    k_rows = ints.shape[0]
    whole = jnp.zeros((len(blocks) * k_rows,) + ints.shape[1:], ints.dtype)
    for u, blk in enumerate(blocks):
        whole = lax.dynamic_update_slice_in_dim(whole, blk, (row_at ^ u) * k_rows, axis=0)
    return whole


def ring_reduce_y(part, slab_at, split_axis):
    ny = lax.axis_size("slab") // 2
    width = part.shape[2] // ny
    y_at = slab_at // 2
    half = part.shape[split_axis] // 2
    halves = tuple(lax.slice_in_dim(part, h * half, (h + 1) * half, axis=split_axis) for h in range(2))
    dirs = (1, -1)
    acc = [None, None]
    for step in range(ny - 1):
        for h in range(2):
            d = dirs[h]
            chunk = (y_at - d * (step + 1)) % ny
            own = lax.dynamic_slice_in_dim(halves[h], chunk * width, width, axis=2)
            send = own if acc[h] is None else acc[h] + own
            acc[h] = shifted(send, "slab", lambda s, d=d: s + 2 * d)
    result = []
    for h in range(2):
        own = lax.dynamic_slice_in_dim(halves[h], y_at * width, width, axis=2)
        result.append(acc[h] + own)
    return jnp.concatenate(result, axis=split_axis)


def body(amplitudes, integrals, irreps, pair_mask):
    i_rows, k_rows, c_cols, win_cols = amplitudes.shape
    blocks = pair_mask.shape[0]
    row_at = lax.axis_index("row")
    col_at = lax.axis_index("col")
    slab_at = lax.axis_index("slab")
    n_slab = lax.axis_size("slab")

    keep = pair_mask[row_at, col_at] != 0
    amp = jnp.where(keep, amplitudes, jnp.zeros_like(amplitudes))
    mask = int_mask(irreps, blocks, row_at, col_at, slab_at, c_cols, win_cols)
    ints = jnp.where(mask[None, :, None, :], integrals, jnp.zeros_like(integrals))

    amp_all = lax.all_gather(amp, "col", axis=1, tiled=True)
    int_abs = gather_row(ints, row_at)
    n_row = lax.axis_size("row")
    n_col = lax.axis_size("col")
    n_chunks = 2
    rows = i_rows // n_chunks
    share_parts = []
    mirror_parts = []
    for ch in range(n_chunks):
        amp_part = lax.slice_in_dim(amp_all, ch * rows, (ch + 1) * rows, axis=0)
        part = jnp.einsum("ikca,kcjb->ijab", amp_part, int_abs, preferred_element_type=jnp.float32)
        reduced_y = ring_reduce_y(part, slab_at, 1)
        zh = slab_at % 2
        width = reduced_y.shape[2] // 2
        mine = lax.dynamic_slice_in_dim(reduced_y, zh * width, width, axis=2)
        theirs = lax.dynamic_slice_in_dim(reduced_y, (1 - zh) * width, width, axis=2)
        shares = mine + shifted(theirs, "slab", lambda s: s ^ 1)
        share_parts.append(shares)

        i_n, j_n, a_n, b_n = shares.shape
        gathered = jnp.zeros((n_slab, j_n * i_n, a_n * a_n), shares.dtype)
        for d in range(n_slab):
            tile = lax.dynamic_slice_in_dim(shares, (slab_at ^ d) * a_n, a_n, axis=3)
            flat = jnp.transpose(tile, (1, 0, 3, 2)).reshape(1, j_n * i_n, a_n * a_n)
            pairs = [
                ((r * n_col + c) * n_slab + t, (c * n_col + r) * n_slab + (t ^ d))
                for r in range(n_row)
                for c in range(n_col)
                for t in range(n_slab)
            ]
            flat = lax.ppermute(flat, ("row", "col", "slab"), pairs)
            gathered = lax.dynamic_update_slice_in_dim(gathered, flat, slab_at ^ d, axis=0)
        gathered = gathered.reshape(n_slab, j_n, i_n, a_n, a_n)
        mirror_parts.append(jnp.transpose(gathered, (1, 2, 3, 0, 4)).reshape(j_n, i_n, a_n, b_n))
    shares = jnp.concatenate(share_parts, axis=0)
    mirrored = jnp.concatenate(mirror_parts, axis=1)
    return (shares + mirrored).astype(jnp.bfloat16)


def solution(mesh):
    return jax.shard_map(
        body,
        mesh=mesh,
        in_specs=(P("row", "col", "slab", None), P("row", "slab", "col", None), P(), P()),
        out_specs=P("row", "col", "slab", None),
        check_vma=False,
    )
```

```python
import jax
import jax.numpy as jnp
from jax import lax
from jax.sharding import PartitionSpec as P

OBLK = 12
VTILE = 32


def shifted(value, axis, fn):
    size = lax.axis_size(axis)
    return lax.ppermute(value, axis, [(src, fn(src) % size) for src in range(size)])


def int_mask(irreps, blocks, row_at, col_at, slab_at, c_cols, win_cols):
    c_ids = slab_at * c_cols + jnp.arange(c_cols, dtype=jnp.int32)
    b_ids = jnp.arange(win_cols, dtype=jnp.int32)
    label_c = jnp.take(irreps, blocks + c_ids // VTILE)
    label_b = jnp.take(irreps, blocks + b_ids // VTILE)
    occ = irreps[row_at] + irreps[col_at]
    parity = occ + label_c[:, None] + label_b[None, :]
    return parity % 2 == 0


def gather_row(ints, row_at):
    zpart = shifted(ints, "row", lambda r: r ^ 2)
    blocks = [ints, shifted(ints, "row", lambda r: r ^ 1), zpart, shifted(zpart, "row", lambda r: r ^ 1)]
    k_rows = ints.shape[0]
    whole = jnp.zeros((len(blocks) * k_rows,) + ints.shape[1:], ints.dtype)
    for u, blk in enumerate(blocks):
        whole = lax.dynamic_update_slice_in_dim(whole, blk, (row_at ^ u) * k_rows, axis=0)
    return whole


def ring_reduce_y(part, slab_at, split_axis):
    ny = lax.axis_size("slab") // 2
    width = part.shape[2] // ny
    y_at = slab_at // 2
    half = part.shape[split_axis] // 2
    halves = tuple(lax.slice_in_dim(part, h * half, (h + 1) * half, axis=split_axis) for h in range(2))
    dirs = (1, -1)
    acc = [None, None]
    for step in range(ny - 1):
        for h in range(2):
            d = dirs[h]
            chunk = (y_at - d * (step + 1)) % ny
            own = lax.dynamic_slice_in_dim(halves[h], chunk * width, width, axis=2)
            send = own if acc[h] is None else acc[h] + own
            acc[h] = shifted(send, "slab", lambda s, d=d: s + 2 * d)
    result = []
    for h in range(2):
        own = lax.dynamic_slice_in_dim(halves[h], y_at * width, width, axis=2)
        result.append(acc[h] + own)
    return jnp.concatenate(result, axis=split_axis)


def body(amplitudes, integrals, irreps, pair_mask):
    i_rows, k_rows, c_cols, win_cols = amplitudes.shape
    blocks = pair_mask.shape[0]
    row_at = lax.axis_index("row")
    col_at = lax.axis_index("col")
    slab_at = lax.axis_index("slab")
    n_slab = lax.axis_size("slab")

    keep = pair_mask[row_at, col_at] != 0
    amp = jnp.where(keep, amplitudes, jnp.zeros_like(amplitudes))
    mask = int_mask(irreps, blocks, row_at, col_at, slab_at, c_cols, win_cols)
    ints = jnp.where(mask[None, :, None, :], integrals, jnp.zeros_like(integrals))

    amp_all = lax.all_gather(amp, "col", axis=1, tiled=True)
    int_abs = gather_row(ints, row_at)
    n_row = lax.axis_size("row")
    n_col = lax.axis_size("col")
    n_chunks = 2
    rows = i_rows // n_chunks
    share_parts = []
    for ch in range(n_chunks):
        amp_part = lax.slice_in_dim(amp_all, ch * rows, (ch + 1) * rows, axis=0)
        part = jnp.einsum("ikca,kcjb->ijab", amp_part, int_abs, preferred_element_type=jnp.float32)
        reduced_y = ring_reduce_y(part, slab_at, 1)
        zh = slab_at % 2
        width = reduced_y.shape[2] // 2
        mine = lax.dynamic_slice_in_dim(reduced_y, zh * width, width, axis=2)
        theirs = lax.dynamic_slice_in_dim(reduced_y, (1 - zh) * width, width, axis=2)
        shares = mine + shifted(theirs, "slab", lambda s: s ^ 1)
        share_parts.append(shares)
    shares = jnp.concatenate(share_parts, axis=0)

    i_n, j_n, a_n, b_n = shares.shape
    gathered = jnp.zeros((n_slab, j_n * i_n, a_n * a_n), shares.dtype)
    for d in range(n_slab):
        tile = lax.dynamic_slice_in_dim(shares, (slab_at ^ d) * a_n, a_n, axis=3)
        flat = jnp.transpose(tile, (1, 0, 3, 2)).reshape(1, j_n * i_n, a_n * a_n)
        pairs = [
            ((r * n_col + c) * n_slab + t, (c * n_col + r) * n_slab + (t ^ d))
            for r in range(n_row)
            for c in range(n_col)
            for t in range(n_slab)
        ]
        flat = lax.ppermute(flat, ("row", "col", "slab"), pairs)
        gathered = lax.dynamic_update_slice_in_dim(gathered, flat, slab_at ^ d, axis=0)
    gathered = gathered.reshape(n_slab, j_n, i_n, a_n, a_n)
    mirrored = jnp.transpose(gathered, (1, 2, 3, 0, 4)).reshape(shares.shape)
    return (shares + mirrored).astype(jnp.bfloat16)


def solution(mesh):
    return jax.shard_map(
        body,
        mesh=mesh,
        in_specs=(P("row", "col", "slab", None), P("row", "slab", "col", None), P(), P()),
        out_specs=P("row", "col", "slab", None),
        check_vma=False,
    )
```

```python
import jax
import jax.numpy as jnp
from jax import lax
from jax.sharding import PartitionSpec as P

OBLK = 12
VTILE = 32


def shifted(value, axis, fn):
    size = lax.axis_size(axis)
    return lax.ppermute(value, axis, [(src, fn(src) % size) for src in range(size)])


def int_mask(irreps, blocks, row_at, col_at, slab_at, c_cols, win_cols):
    c_ids = slab_at * c_cols + jnp.arange(c_cols, dtype=jnp.int32)
    b_ids = jnp.arange(win_cols, dtype=jnp.int32)
    label_c = jnp.take(irreps, blocks + c_ids // VTILE)
    label_b = jnp.take(irreps, blocks + b_ids // VTILE)
    occ = irreps[row_at] + irreps[col_at]
    parity = occ + label_c[:, None] + label_b[None, :]
    return parity % 2 == 0


def gather_row(ints, row_at):
    zpart = shifted(ints, "row", lambda r: r ^ 2)
    blocks = [ints, shifted(ints, "row", lambda r: r ^ 1), zpart, shifted(zpart, "row", lambda r: r ^ 1)]
    k_rows = ints.shape[0]
    whole = jnp.zeros((len(blocks) * k_rows,) + ints.shape[1:], ints.dtype)
    for u, blk in enumerate(blocks):
        whole = lax.dynamic_update_slice_in_dim(whole, blk, (row_at ^ u) * k_rows, axis=0)
    return whole


def ring_reduce_y(part, slab_at, split_axis):
    ny = lax.axis_size("slab") // 2
    width = part.shape[2] // ny
    y_at = slab_at // 2
    half = part.shape[split_axis] // 2
    halves = tuple(lax.slice_in_dim(part, h * half, (h + 1) * half, axis=split_axis) for h in range(2))
    dirs = (1, -1)
    acc = [None, None]
    for step in range(ny - 1):
        for h in range(2):
            d = dirs[h]
            chunk = (y_at - d * (step + 1)) % ny
            own = lax.dynamic_slice_in_dim(halves[h], chunk * width, width, axis=2)
            send = own if acc[h] is None else acc[h] + own
            acc[h] = shifted(send, "slab", lambda s, d=d: s + 2 * d)
    result = []
    for h in range(2):
        own = lax.dynamic_slice_in_dim(halves[h], y_at * width, width, axis=2)
        result.append(acc[h] + own)
    return jnp.concatenate(result, axis=split_axis)


def body(amplitudes, integrals, irreps, pair_mask):
    i_rows, k_rows, c_cols, win_cols = amplitudes.shape
    blocks = pair_mask.shape[0]
    row_at = lax.axis_index("row")
    col_at = lax.axis_index("col")
    slab_at = lax.axis_index("slab")
    n_slab = lax.axis_size("slab")

    keep = pair_mask[row_at, col_at] != 0
    amp = jnp.where(keep, amplitudes, jnp.zeros_like(amplitudes))
    mask = int_mask(irreps, blocks, row_at, col_at, slab_at, c_cols, win_cols)
    ints = jnp.where(mask[None, :, None, :], integrals, jnp.zeros_like(integrals))

    amp_all = lax.all_gather(amp, "col", axis=1, tiled=True)
    int_abs = gather_row(ints, row_at)
    n_row = lax.axis_size("row")
    n_col = lax.axis_size("col")
    n_chunks = 2
    rows = i_rows // n_chunks
    share_parts = []
    for ch in range(n_chunks):
        amp_part = lax.slice_in_dim(amp_all, ch * rows, (ch + 1) * rows, axis=0)
        part = jnp.einsum("ikca,kcjb->ijab", amp_part, int_abs, preferred_element_type=jnp.float32)
        reduced_y = ring_reduce_y(part, slab_at, 1)
        zh = slab_at % 2
        width = reduced_y.shape[2] // 2
        mine = lax.dynamic_slice_in_dim(reduced_y, zh * width, width, axis=2)
        theirs = lax.dynamic_slice_in_dim(reduced_y, (1 - zh) * width, width, axis=2)
        shares = mine + shifted(theirs, "slab", lambda s: s ^ 1)
        share_parts.append(shares)
    shares = jnp.concatenate(share_parts, axis=0)

    i_n, j_n, a_n, b_n = shares.shape
    outgoing = jnp.transpose(shares.reshape(i_n, j_n, a_n, n_slab, b_n // n_slab), (3, 1, 0, 4, 2))
    outgoing = outgoing.reshape(n_slab, j_n * i_n, a_n * a_n)
    gathered = jnp.zeros((n_slab, j_n * i_n, a_n * a_n), shares.dtype)
    for d in range(n_slab):
        flat = lax.dynamic_slice_in_dim(outgoing, slab_at ^ d, 1, axis=0)
        pairs = [
            ((r * n_col + c) * n_slab + t, (c * n_col + r) * n_slab + (t ^ d))
            for r in range(n_row)
            for c in range(n_col)
            for t in range(n_slab)
        ]
        flat = lax.ppermute(flat, ("row", "col", "slab"), pairs)
        gathered = lax.dynamic_update_slice_in_dim(gathered, flat, slab_at ^ d, axis=0)
    gathered = gathered.reshape(n_slab, j_n, i_n, a_n, a_n)
    mirrored = jnp.transpose(gathered, (1, 2, 3, 0, 4)).reshape(shares.shape)
    return (shares + mirrored).astype(jnp.bfloat16)


def solution(mesh):
    return jax.shard_map(
        body,
        mesh=mesh,
        in_specs=(P("row", "col", "slab", None), P("row", "slab", "col", None), P(), P()),
        out_specs=P("row", "col", "slab", None),
        check_vma=False,
    )
```

```python
import jax
import jax.numpy as jnp
from jax import lax
from jax.sharding import PartitionSpec as P

OBLK = 12
VTILE = 32


def shifted(value, axis, fn):
    size = lax.axis_size(axis)
    return lax.ppermute(value, axis, [(src, fn(src) % size) for src in range(size)])


def int_mask(irreps, blocks, k_block, col_at, slab_at, c_cols, win_cols):
    c_ids = slab_at * c_cols + jnp.arange(c_cols, dtype=jnp.int32)
    b_ids = jnp.arange(win_cols, dtype=jnp.int32)
    label_c = jnp.take(irreps, blocks + c_ids // VTILE)
    label_b = jnp.take(irreps, blocks + b_ids // VTILE)
    occ = irreps[k_block] + irreps[col_at]
    parity = occ + label_c[:, None] + label_b[None, :]
    return parity % 2 == 0


def gather_row(ints, row_at, block_mask):
    zpart = shifted(ints, "row", lambda r: r ^ 2)
    blocks = [ints, shifted(ints, "row", lambda r: r ^ 1), zpart, shifted(zpart, "row", lambda r: r ^ 1)]
    k_rows = ints.shape[0]
    whole = jnp.zeros((len(blocks) * k_rows,) + ints.shape[1:], ints.dtype)
    for u, blk in enumerate(blocks):
        mask = block_mask(row_at ^ u)
        blk = jnp.where(mask[None, :, None, :], blk, jnp.zeros_like(blk))
        whole = lax.dynamic_update_slice_in_dim(whole, blk, (row_at ^ u) * k_rows, axis=0)
    return whole


def ring_reduce_y(part, slab_at, split_axis):
    ny = lax.axis_size("slab") // 2
    width = part.shape[2] // ny
    y_at = slab_at // 2
    half = part.shape[split_axis] // 2
    halves = tuple(lax.slice_in_dim(part, h * half, (h + 1) * half, axis=split_axis) for h in range(2))
    dirs = (1, -1)
    acc = [None, None]
    for step in range(ny - 1):
        for h in range(2):
            d = dirs[h]
            chunk = (y_at - d * (step + 1)) % ny
            own = lax.dynamic_slice_in_dim(halves[h], chunk * width, width, axis=2)
            send = own if acc[h] is None else acc[h] + own
            acc[h] = shifted(send, "slab", lambda s, d=d: s + 2 * d)
    result = []
    for h in range(2):
        own = lax.dynamic_slice_in_dim(halves[h], y_at * width, width, axis=2)
        result.append(acc[h] + own)
    return jnp.concatenate(result, axis=split_axis)


def body(amplitudes, integrals, irreps, pair_mask):
    i_rows, k_rows, c_cols, win_cols = amplitudes.shape
    blocks = pair_mask.shape[0]
    row_at = lax.axis_index("row")
    col_at = lax.axis_index("col")
    slab_at = lax.axis_index("slab")
    n_slab = lax.axis_size("slab")

    keep = pair_mask[row_at, col_at] != 0
    amp = jnp.where(keep, amplitudes, jnp.zeros_like(amplitudes))
    amp_all = lax.all_gather(amp, "col", axis=1, tiled=True)

    def block_mask(k_block):
        return int_mask(irreps, blocks, k_block, col_at, slab_at, c_cols, win_cols)

    int_abs = gather_row(integrals, row_at, block_mask)
    n_row = lax.axis_size("row")
    n_col = lax.axis_size("col")
    n_chunks = 2
    rows = i_rows // n_chunks
    share_parts = []
    for ch in range(n_chunks):
        amp_part = lax.slice_in_dim(amp_all, ch * rows, (ch + 1) * rows, axis=0)
        part = jnp.einsum("ikca,kcjb->ijab", amp_part, int_abs, preferred_element_type=jnp.float32)
        reduced_y = ring_reduce_y(part, slab_at, 1)
        zh = slab_at % 2
        width = reduced_y.shape[2] // 2
        mine = lax.dynamic_slice_in_dim(reduced_y, zh * width, width, axis=2)
        theirs = lax.dynamic_slice_in_dim(reduced_y, (1 - zh) * width, width, axis=2)
        shares = mine + shifted(theirs, "slab", lambda s: s ^ 1)
        share_parts.append(shares)
    shares = jnp.concatenate(share_parts, axis=0)

    i_n, j_n, a_n, b_n = shares.shape
    outgoing = jnp.transpose(shares.reshape(i_n, j_n, a_n, n_slab, b_n // n_slab), (3, 1, 0, 4, 2))
    outgoing = outgoing.reshape(n_slab, j_n * i_n, a_n * a_n)
    gathered = jnp.zeros((n_slab, j_n * i_n, a_n * a_n), shares.dtype)
    for d in range(n_slab):
        flat = lax.dynamic_slice_in_dim(outgoing, slab_at ^ d, 1, axis=0)
        pairs = [
            ((r * n_col + c) * n_slab + t, (c * n_col + r) * n_slab + (t ^ d))
            for r in range(n_row)
            for c in range(n_col)
            for t in range(n_slab)
        ]
        flat = lax.ppermute(flat, ("row", "col", "slab"), pairs)
        gathered = lax.dynamic_update_slice_in_dim(gathered, flat, slab_at ^ d, axis=0)
    gathered = gathered.reshape(n_slab, j_n, i_n, a_n, a_n)
    mirrored = jnp.transpose(gathered, (1, 2, 3, 0, 4)).reshape(shares.shape)
    return (shares + mirrored).astype(jnp.bfloat16)


def solution(mesh):
    return jax.shard_map(
        body,
        mesh=mesh,
        in_specs=(P("row", "col", "slab", None), P("row", "slab", "col", None), P(), P()),
        out_specs=P("row", "col", "slab", None),
        check_vma=False,
    )
```

```python
import jax
import jax.numpy as jnp
from jax import lax
from jax.sharding import PartitionSpec as P

OBLK = 12
VTILE = 32


def shifted(value, axis, fn):
    size = lax.axis_size(axis)
    return lax.ppermute(value, axis, [(src, fn(src) % size) for src in range(size)])


def int_mask(irreps, blocks, row_at, col_at, slab_at, c_cols, win_cols):
    c_ids = slab_at * c_cols + jnp.arange(c_cols, dtype=jnp.int32)
    b_ids = jnp.arange(win_cols, dtype=jnp.int32)
    label_c = jnp.take(irreps, blocks + c_ids // VTILE)
    label_b = jnp.take(irreps, blocks + b_ids // VTILE)
    occ = irreps[row_at] + irreps[col_at]
    parity = occ + label_c[:, None] + label_b[None, :]
    return parity % 2 == 0


def gather_row(ints, row_at):
    zpart = shifted(ints, "row", lambda r: r ^ 2)
    blocks = [ints, shifted(ints, "row", lambda r: r ^ 1), zpart, shifted(zpart, "row", lambda r: r ^ 1)]
    k_rows = ints.shape[0]
    whole = jnp.zeros((len(blocks) * k_rows,) + ints.shape[1:], ints.dtype)
    for u, blk in enumerate(blocks):
        whole = lax.dynamic_update_slice_in_dim(whole, blk, (row_at ^ u) * k_rows, axis=0)
    return whole


def gather_col_rows(amp, col_at):
    near1 = shifted(amp, "col", lambda c: c ^ 1)
    near3 = shifted(amp, "col", lambda c: c ^ 3)
    half = amp.shape[0] // 2
    far_a = shifted(near3[:half], "col", lambda c: c ^ 1)
    far_b = shifted(near1[half:], "col", lambda c: c ^ 3)
    far = jnp.concatenate([far_a, far_b], axis=0)
    k_rows = amp.shape[1]
    whole = jnp.zeros((amp.shape[0], 4 * k_rows) + amp.shape[2:], amp.dtype)
    for v, blk in enumerate([amp, near1, far, near3]):
        whole = lax.dynamic_update_slice_in_dim(whole, blk, (col_at ^ v) * k_rows, axis=1)
    return whole


def ring_reduce_y(part, slab_at, split_axis):
    ny = lax.axis_size("slab") // 2
    width = part.shape[2] // ny
    y_at = slab_at // 2
    half = part.shape[split_axis] // 2
    halves = tuple(lax.slice_in_dim(part, h * half, (h + 1) * half, axis=split_axis) for h in range(2))
    dirs = (1, -1)
    acc = [None, None]
    for step in range(ny - 1):
        for h in range(2):
            d = dirs[h]
            chunk = (y_at - d * (step + 1)) % ny
            own = lax.dynamic_slice_in_dim(halves[h], chunk * width, width, axis=2)
            send = own if acc[h] is None else acc[h] + own
            acc[h] = shifted(send, "slab", lambda s, d=d: s + 2 * d)
    result = []
    for h in range(2):
        own = lax.dynamic_slice_in_dim(halves[h], y_at * width, width, axis=2)
        result.append(acc[h] + own)
    return jnp.concatenate(result, axis=split_axis)


def body(amplitudes, integrals, irreps, pair_mask):
    i_rows, k_rows, c_cols, win_cols = amplitudes.shape
    blocks = pair_mask.shape[0]
    row_at = lax.axis_index("row")
    col_at = lax.axis_index("col")
    slab_at = lax.axis_index("slab")
    n_slab = lax.axis_size("slab")

    keep = pair_mask[row_at, col_at] != 0
    amp = jnp.where(keep, amplitudes, jnp.zeros_like(amplitudes))
    mask = int_mask(irreps, blocks, row_at, col_at, slab_at, c_cols, win_cols)
    ints = jnp.where(mask[None, :, None, :], integrals, jnp.zeros_like(integrals))

    sc_rows = 2 * i_rows // 3
    amp_all = jnp.concatenate(
        [
            lax.all_gather(amp[:sc_rows], "col", axis=1, tiled=True),
            gather_col_rows(amp[sc_rows:], col_at),
        ],
        axis=0,
    )
    int_abs = gather_row(ints, row_at)
    n_row = lax.axis_size("row")
    n_col = lax.axis_size("col")
    n_chunks = 2
    rows = i_rows // n_chunks
    share_parts = []
    for ch in range(n_chunks):
        amp_part = lax.slice_in_dim(amp_all, ch * rows, (ch + 1) * rows, axis=0)
        part = jnp.einsum("ikca,kcjb->ijab", amp_part, int_abs, preferred_element_type=jnp.float32)
        reduced_y = ring_reduce_y(part, slab_at, 1)
        zh = slab_at % 2
        width = reduced_y.shape[2] // 2
        mine = lax.dynamic_slice_in_dim(reduced_y, zh * width, width, axis=2)
        theirs = lax.dynamic_slice_in_dim(reduced_y, (1 - zh) * width, width, axis=2)
        shares = mine + shifted(theirs, "slab", lambda s: s ^ 1)
        share_parts.append(shares)
    shares = jnp.concatenate(share_parts, axis=0)

    i_n, j_n, a_n, b_n = shares.shape
    outgoing = jnp.transpose(shares.reshape(i_n, j_n, a_n, n_slab, b_n // n_slab), (3, 1, 0, 4, 2))
    outgoing = outgoing.reshape(n_slab, j_n * i_n, a_n * a_n)
    gathered = jnp.zeros((n_slab, j_n * i_n, a_n * a_n), shares.dtype)
    for d in range(n_slab):
        flat = lax.dynamic_slice_in_dim(outgoing, slab_at ^ d, 1, axis=0)
        pairs = [
            ((r * n_col + c) * n_slab + t, (c * n_col + r) * n_slab + (t ^ d))
            for r in range(n_row)
            for c in range(n_col)
            for t in range(n_slab)
        ]
        flat = lax.ppermute(flat, ("row", "col", "slab"), pairs)
        gathered = lax.dynamic_update_slice_in_dim(gathered, flat, slab_at ^ d, axis=0)
    gathered = gathered.reshape(n_slab, j_n, i_n, a_n, a_n)
    mirrored = jnp.transpose(gathered, (1, 2, 3, 0, 4)).reshape(shares.shape)
    return (shares + mirrored).astype(jnp.bfloat16)


def solution(mesh):
    return jax.shard_map(
        body,
        mesh=mesh,
        in_specs=(P("row", "col", "slab", None), P("row", "slab", "col", None), P(), P()),
        out_specs=P("row", "col", "slab", None),
        check_vma=False,
    )
```

```python
import jax
import jax.numpy as jnp
from jax import lax
from jax.sharding import PartitionSpec as P

OBLK = 12
VTILE = 32


def shifted(value, axis, fn):
    size = lax.axis_size(axis)
    return lax.ppermute(value, axis, [(src, fn(src) % size) for src in range(size)])


def int_mask(irreps, blocks, row_at, col_at, slab_at, c_cols, win_cols):
    c_ids = slab_at * c_cols + jnp.arange(c_cols, dtype=jnp.int32)
    b_ids = jnp.arange(win_cols, dtype=jnp.int32)
    label_c = jnp.take(irreps, blocks + c_ids // VTILE)
    label_b = jnp.take(irreps, blocks + b_ids // VTILE)
    occ = irreps[row_at] + irreps[col_at]
    parity = occ + label_c[:, None] + label_b[None, :]
    return parity % 2 == 0


def gather_row(ints, row_at):
    zpart = shifted(ints, "row", lambda r: r ^ 2)
    blocks = [ints, shifted(ints, "row", lambda r: r ^ 1), zpart, shifted(zpart, "row", lambda r: r ^ 1)]
    k_rows = ints.shape[0]
    whole = jnp.zeros((len(blocks) * k_rows,) + ints.shape[1:], ints.dtype)
    for u, blk in enumerate(blocks):
        whole = lax.dynamic_update_slice_in_dim(whole, blk, (row_at ^ u) * k_rows, axis=0)
    return whole


def ring_reduce_y(part, slab_at, split_axis):
    ny = lax.axis_size("slab") // 2
    width = part.shape[2] // ny
    y_at = slab_at // 2
    half = part.shape[split_axis] // 2
    halves = tuple(lax.slice_in_dim(part, h * half, (h + 1) * half, axis=split_axis) for h in range(2))
    dirs = (1, -1)
    acc = [None, None]
    for step in range(ny - 1):
        for h in range(2):
            d = dirs[h]
            chunk = (y_at - d * (step + 1)) % ny
            own = lax.dynamic_slice_in_dim(halves[h], chunk * width, width, axis=2)
            send = own if acc[h] is None else acc[h] + own
            acc[h] = shifted(send, "slab", lambda s, d=d: s + 2 * d)
    result = []
    for h in range(2):
        own = lax.dynamic_slice_in_dim(halves[h], y_at * width, width, axis=2)
        result.append(acc[h] + own)
    return jnp.concatenate(result, axis=split_axis)


def body(amplitudes, integrals, irreps, pair_mask):
    i_rows, k_rows, c_cols, win_cols = amplitudes.shape
    blocks = pair_mask.shape[0]
    row_at = lax.axis_index("row")
    col_at = lax.axis_index("col")
    slab_at = lax.axis_index("slab")
    n_slab = lax.axis_size("slab")

    keep = pair_mask[row_at, col_at] != 0
    amp = jnp.where(keep, amplitudes, jnp.zeros_like(amplitudes))
    mask = int_mask(irreps, blocks, row_at, col_at, slab_at, c_cols, win_cols)
    ints = jnp.where(mask[None, :, None, :], integrals, jnp.zeros_like(integrals))

    amp_all = lax.all_gather(amp, "col", axis=1, tiled=True)
    int_abs = gather_row(ints, row_at)
    n_row = lax.axis_size("row")
    n_col = lax.axis_size("col")
    n_chunks = 2
    rows = i_rows // n_chunks
    share_parts = []
    for ch in range(n_chunks):
        amp_part = lax.slice_in_dim(amp_all, ch * rows, (ch + 1) * rows, axis=0)
        part = jnp.einsum("ikca,kcjb->ijab", amp_part, int_abs, preferred_element_type=jnp.float32)
        reduced_y = ring_reduce_y(part, slab_at, 1)
        zh = slab_at % 2
        width = reduced_y.shape[2] // 2
        mine = lax.dynamic_slice_in_dim(reduced_y, zh * width, width, axis=2)
        theirs = lax.dynamic_slice_in_dim(reduced_y, (1 - zh) * width, width, axis=2)
        shares = mine + shifted(theirs, "slab", lambda s: s ^ 1)
        share_parts.append(shares)
    shares = jnp.concatenate(share_parts, axis=0)

    i_n, j_n, a_n, b_n = shares.shape
    outgoing = jnp.transpose(shares.reshape(i_n, j_n, a_n, n_slab, b_n // n_slab), (3, 1, 0, 4, 2))
    outgoing = outgoing.reshape(n_slab, j_n * i_n, a_n * a_n)
    gathered = jnp.zeros((n_slab, j_n * i_n, a_n * a_n), shares.dtype)
    for d in range(n_slab):
        flat = lax.dynamic_slice_in_dim(outgoing, slab_at ^ d, 1, axis=0)
        pairs = [
            ((r * n_col + c) * n_slab + t, (c * n_col + r) * n_slab + (t ^ d))
            for r in range(n_row)
            for c in range(n_col)
            for t in range(n_slab)
        ]
        flat = lax.ppermute(flat, ("row", "col", "slab"), pairs)
        gathered = lax.dynamic_update_slice_in_dim(gathered, flat, slab_at ^ d, axis=0)
    gathered = gathered.reshape(n_slab, j_n, i_n, a_n, a_n)
    mirrored = jnp.transpose(gathered, (1, 2, 3, 0, 4))
    total = shares.reshape(mirrored.shape) + mirrored
    return total.astype(jnp.bfloat16).reshape(shares.shape)


def solution(mesh):
    return jax.shard_map(
        body,
        mesh=mesh,
        in_specs=(P("row", "col", "slab", None), P("row", "slab", "col", None), P(), P()),
        out_specs=P("row", "col", "slab", None),
        check_vma=False,
    )
```

```python
import jax
import jax.numpy as jnp
from jax import lax
from jax.sharding import PartitionSpec as P

OBLK = 12
VTILE = 32


def shifted(value, axis, fn):
    size = lax.axis_size(axis)
    return lax.ppermute(value, axis, [(src, fn(src) % size) for src in range(size)])


def int_mask(irreps, blocks, row_at, col_at, slab_at, c_cols, win_cols):
    c_ids = slab_at * c_cols + jnp.arange(c_cols, dtype=jnp.int32)
    b_ids = jnp.arange(win_cols, dtype=jnp.int32)
    label_c = jnp.take(irreps, blocks + c_ids // VTILE)
    label_b = jnp.take(irreps, blocks + b_ids // VTILE)
    occ = irreps[row_at] + irreps[col_at]
    parity = occ + label_c[:, None] + label_b[None, :]
    return parity % 2 == 0


def gather_row(ints, row_at):
    zpart = shifted(ints, "row", lambda r: r ^ 2)
    blocks = [ints, shifted(ints, "row", lambda r: r ^ 1), zpart, shifted(zpart, "row", lambda r: r ^ 1)]
    k_rows = ints.shape[0]
    whole = jnp.zeros((len(blocks) * k_rows,) + ints.shape[1:], ints.dtype)
    for u, blk in enumerate(blocks):
        whole = lax.dynamic_update_slice_in_dim(whole, blk, (row_at ^ u) * k_rows, axis=0)
    return whole


def ring_reduce_y(part, slab_at, split_axis):
    ny = lax.axis_size("slab") // 2
    width = part.shape[2] // ny
    y_at = slab_at // 2
    half = part.shape[split_axis] // 2
    halves = tuple(lax.slice_in_dim(part, h * half, (h + 1) * half, axis=split_axis) for h in range(2))
    dirs = (1, -1)
    acc = [None, None]
    for step in range(ny - 1):
        for h in range(2):
            d = dirs[h]
            chunk = (y_at - d * (step + 1)) % ny
            own = lax.dynamic_slice_in_dim(halves[h], chunk * width, width, axis=2)
            send = own if acc[h] is None else acc[h] + own
            acc[h] = shifted(send, "slab", lambda s, d=d: s + 2 * d)
    result = []
    for h in range(2):
        own = lax.dynamic_slice_in_dim(halves[h], y_at * width, width, axis=2)
        result.append(acc[h] + own)
    return jnp.concatenate(result, axis=split_axis)


def body(amplitudes, integrals, irreps, pair_mask):
    i_rows, k_rows, c_cols, win_cols = amplitudes.shape
    blocks = pair_mask.shape[0]
    row_at = lax.axis_index("row")
    col_at = lax.axis_index("col")
    slab_at = lax.axis_index("slab")
    n_slab = lax.axis_size("slab")

    keep = pair_mask[row_at, col_at] != 0
    amp = jnp.where(keep, amplitudes, jnp.zeros_like(amplitudes))
    mask = int_mask(irreps, blocks, row_at, col_at, slab_at, c_cols, win_cols)
    ints = jnp.where(mask[None, :, None, :], integrals, jnp.zeros_like(integrals))

    amp_all = lax.all_gather(amp, "col", axis=1, tiled=True)
    int_abs = gather_row(ints, row_at)
    n_row = lax.axis_size("row")
    n_col = lax.axis_size("col")
    n_chunks = 3
    rows = i_rows // n_chunks
    share_parts = []
    for ch in range(n_chunks):
        amp_part = lax.slice_in_dim(amp_all, ch * rows, (ch + 1) * rows, axis=0)
        part = jnp.einsum("ikca,kcjb->ijab", amp_part, int_abs, preferred_element_type=jnp.float32)
        reduced_y = ring_reduce_y(part, slab_at, 1)
        zh = slab_at % 2
        width = reduced_y.shape[2] // 2
        mine = lax.dynamic_slice_in_dim(reduced_y, zh * width, width, axis=2)
        theirs = lax.dynamic_slice_in_dim(reduced_y, (1 - zh) * width, width, axis=2)
        shares = mine + shifted(theirs, "slab", lambda s: s ^ 1)
        share_parts.append(shares)
    shares = jnp.concatenate(share_parts, axis=0)

    i_n, j_n, a_n, b_n = shares.shape
    outgoing = jnp.transpose(shares.reshape(i_n, j_n, a_n, n_slab, b_n // n_slab), (3, 1, 0, 4, 2))
    outgoing = outgoing.reshape(n_slab, j_n * i_n, a_n * a_n)
    gathered = jnp.zeros((n_slab, j_n * i_n, a_n * a_n), shares.dtype)
    for d in range(n_slab):
        flat = lax.dynamic_slice_in_dim(outgoing, slab_at ^ d, 1, axis=0)
        pairs = [
            ((r * n_col + c) * n_slab + t, (c * n_col + r) * n_slab + (t ^ d))
            for r in range(n_row)
            for c in range(n_col)
            for t in range(n_slab)
        ]
        flat = lax.ppermute(flat, ("row", "col", "slab"), pairs)
        gathered = lax.dynamic_update_slice_in_dim(gathered, flat, slab_at ^ d, axis=0)
    gathered = gathered.reshape(n_slab, j_n, i_n, a_n, a_n)
    mirrored = jnp.transpose(gathered, (1, 2, 3, 0, 4)).reshape(shares.shape)
    return (shares + mirrored).astype(jnp.bfloat16)


def solution(mesh):
    return jax.shard_map(
        body,
        mesh=mesh,
        in_specs=(P("row", "col", "slab", None), P("row", "slab", "col", None), P(), P()),
        out_specs=P("row", "col", "slab", None),
        check_vma=False,
    )
```

```python
import jax
import jax.numpy as jnp
from jax import lax
from jax.sharding import PartitionSpec as P

OBLK = 12
VTILE = 32


def shifted(value, axis, fn):
    size = lax.axis_size(axis)
    return lax.ppermute(value, axis, [(src, fn(src) % size) for src in range(size)])


def int_mask(irreps, blocks, row_at, col_at, slab_at, c_cols, win_cols):
    c_ids = slab_at * c_cols + jnp.arange(c_cols, dtype=jnp.int32)
    b_ids = jnp.arange(win_cols, dtype=jnp.int32)
    label_c = jnp.take(irreps, blocks + c_ids // VTILE)
    label_b = jnp.take(irreps, blocks + b_ids // VTILE)
    occ = irreps[row_at] + irreps[col_at]
    parity = occ + label_c[:, None] + label_b[None, :]
    return parity % 2 == 0


def gather_row(ints, row_at):
    zpart = shifted(ints, "row", lambda r: r ^ 2)
    blocks = [ints, shifted(ints, "row", lambda r: r ^ 1), zpart, shifted(zpart, "row", lambda r: r ^ 1)]
    k_rows = ints.shape[0]
    whole = jnp.zeros((len(blocks) * k_rows,) + ints.shape[1:], ints.dtype)
    for u, blk in enumerate(blocks):
        whole = lax.dynamic_update_slice_in_dim(whole, blk, (row_at ^ u) * k_rows, axis=0)
    return whole


def ring_reduce_y(part, slab_at, split_axis):
    ny = lax.axis_size("slab") // 2
    width = part.shape[2] // ny
    y_at = slab_at // 2
    half = part.shape[split_axis] // 2
    halves = tuple(lax.slice_in_dim(part, h * half, (h + 1) * half, axis=split_axis) for h in range(2))
    dirs = (1, -1)
    acc = [None, None]
    for step in range(ny - 1):
        for h in range(2):
            d = dirs[h]
            chunk = (y_at - d * (step + 1)) % ny
            own = lax.dynamic_slice_in_dim(halves[h], chunk * width, width, axis=2)
            send = own if acc[h] is None else acc[h] + own
            acc[h] = shifted(send, "slab", lambda s, d=d: s + 2 * d)
    result = []
    for h in range(2):
        own = lax.dynamic_slice_in_dim(halves[h], y_at * width, width, axis=2)
        result.append(acc[h] + own)
    return jnp.concatenate(result, axis=split_axis)


def body(amplitudes, integrals, irreps, pair_mask):
    i_rows, k_rows, c_cols, win_cols = amplitudes.shape
    blocks = pair_mask.shape[0]
    row_at = lax.axis_index("row")
    col_at = lax.axis_index("col")
    slab_at = lax.axis_index("slab")
    n_slab = lax.axis_size("slab")

    keep = pair_mask[row_at, col_at] != 0
    amp = jnp.where(keep, amplitudes, jnp.zeros_like(amplitudes))
    mask = int_mask(irreps, blocks, row_at, col_at, slab_at, c_cols, win_cols)
    ints = jnp.where(mask[None, :, None, :], integrals, jnp.zeros_like(integrals))

    amp_all = lax.all_gather(amp, "col", axis=1, tiled=True)
    int_abs = gather_row(ints, row_at)
    n_row = lax.axis_size("row")
    n_col = lax.axis_size("col")
    n_chunks = 4
    rows = i_rows // n_chunks
    share_parts = []
    for ch in range(n_chunks):
        amp_part = lax.slice_in_dim(amp_all, ch * rows, (ch + 1) * rows, axis=0)
        part = jnp.einsum("ikca,kcjb->ijab", amp_part, int_abs, preferred_element_type=jnp.float32)
        reduced_y = ring_reduce_y(part, slab_at, 1)
        zh = slab_at % 2
        width = reduced_y.shape[2] // 2
        mine = lax.dynamic_slice_in_dim(reduced_y, zh * width, width, axis=2)
        theirs = lax.dynamic_slice_in_dim(reduced_y, (1 - zh) * width, width, axis=2)
        shares = mine + shifted(theirs, "slab", lambda s: s ^ 1)
        share_parts.append(shares)
    shares = jnp.concatenate(share_parts, axis=0)

    i_n, j_n, a_n, b_n = shares.shape
    outgoing = jnp.transpose(shares.reshape(i_n, j_n, a_n, n_slab, b_n // n_slab), (3, 1, 0, 4, 2))
    outgoing = outgoing.reshape(n_slab, j_n * i_n, a_n * a_n)
    gathered = jnp.zeros((n_slab, j_n * i_n, a_n * a_n), shares.dtype)
    for d in range(n_slab):
        flat = lax.dynamic_slice_in_dim(outgoing, slab_at ^ d, 1, axis=0)
        pairs = [
            ((r * n_col + c) * n_slab + t, (c * n_col + r) * n_slab + (t ^ d))
            for r in range(n_row)
            for c in range(n_col)
            for t in range(n_slab)
        ]
        flat = lax.ppermute(flat, ("row", "col", "slab"), pairs)
        gathered = lax.dynamic_update_slice_in_dim(gathered, flat, slab_at ^ d, axis=0)
    gathered = gathered.reshape(n_slab, j_n, i_n, a_n, a_n)
    mirrored = jnp.transpose(gathered, (1, 2, 3, 0, 4)).reshape(shares.shape)
    return (shares + mirrored).astype(jnp.bfloat16)


def solution(mesh):
    return jax.shard_map(
        body,
        mesh=mesh,
        in_specs=(P("row", "col", "slab", None), P("row", "slab", "col", None), P(), P()),
        out_specs=P("row", "col", "slab", None),
        check_vma=False,
    )
```

```python
import jax
import jax.numpy as jnp
from jax import lax
from jax.sharding import PartitionSpec as P

OBLK = 12
VTILE = 32


def shifted(value, axis, fn):
    size = lax.axis_size(axis)
    return lax.ppermute(value, axis, [(src, fn(src) % size) for src in range(size)])


def int_mask(irreps, blocks, row_at, col_at, slab_at, c_cols, win_cols):
    c_ids = slab_at * c_cols + jnp.arange(c_cols, dtype=jnp.int32)
    b_ids = jnp.arange(win_cols, dtype=jnp.int32)
    label_c = jnp.take(irreps, blocks + c_ids // VTILE)
    label_b = jnp.take(irreps, blocks + b_ids // VTILE)
    occ = irreps[row_at] + irreps[col_at]
    parity = occ + label_c[:, None] + label_b[None, :]
    return parity % 2 == 0


def gather_row(ints, row_at):
    zpart = shifted(ints, "row", lambda r: r ^ 2)
    blocks = [ints, shifted(ints, "row", lambda r: r ^ 1), zpart, shifted(zpart, "row", lambda r: r ^ 1)]
    k_rows = ints.shape[0]
    whole = jnp.zeros((len(blocks) * k_rows,) + ints.shape[1:], ints.dtype)
    for u, blk in enumerate(blocks):
        whole = lax.dynamic_update_slice_in_dim(whole, blk, (row_at ^ u) * k_rows, axis=0)
    return whole


def ring_reduce_y(part, slab_at, split_axis):
    ny = lax.axis_size("slab") // 2
    width = part.shape[2] // ny
    y_at = slab_at // 2
    half = part.shape[split_axis] // 2
    halves = tuple(lax.slice_in_dim(part, h * half, (h + 1) * half, axis=split_axis) for h in range(2))
    dirs = (1, -1)
    acc = [None, None]
    for step in range(ny - 1):
        for h in range(2):
            d = dirs[h]
            chunk = (y_at - d * (step + 1)) % ny
            own = lax.dynamic_slice_in_dim(halves[h], chunk * width, width, axis=2)
            send = own if acc[h] is None else acc[h] + own
            acc[h] = shifted(send, "slab", lambda s, d=d: s + 2 * d)
    result = []
    for h in range(2):
        own = lax.dynamic_slice_in_dim(halves[h], y_at * width, width, axis=2)
        result.append(acc[h] + own)
    return jnp.concatenate(result, axis=split_axis)


def body(amplitudes, integrals, irreps, pair_mask):
    i_rows, k_rows, c_cols, win_cols = amplitudes.shape
    blocks = pair_mask.shape[0]
    row_at = lax.axis_index("row")
    col_at = lax.axis_index("col")
    slab_at = lax.axis_index("slab")
    n_slab = lax.axis_size("slab")

    keep = pair_mask[row_at, col_at] != 0
    amp = jnp.where(keep, amplitudes, jnp.zeros_like(amplitudes))
    mask = int_mask(irreps, blocks, row_at, col_at, slab_at, c_cols, win_cols)
    ints = jnp.where(mask[None, :, None, :], integrals, jnp.zeros_like(integrals))

    amp_all = lax.all_gather(amp, "col", axis=1, tiled=True)
    int_abs = gather_row(ints, row_at)
    n_row = lax.axis_size("row")
    n_col = lax.axis_size("col")
    n_chunks = 3
    rows = i_rows // n_chunks
    share_parts = []
    for ch in range(n_chunks):
        amp_part = lax.slice_in_dim(amp_all, ch * rows, (ch + 1) * rows, axis=0)
        part = jnp.einsum("ikca,kcjb->ijab", amp_part, int_abs, preferred_element_type=jnp.float32)
        reduced_y = ring_reduce_y(part, slab_at, 1)
        zh = slab_at % 2
        width = reduced_y.shape[2] // 2
        mine = lax.dynamic_slice_in_dim(reduced_y, zh * width, width, axis=2)
        theirs = lax.dynamic_slice_in_dim(reduced_y, (1 - zh) * width, width, axis=2)
        shares = mine + shifted(theirs, "slab", lambda s: s ^ 1)
        share_parts.append(shares)
        c_i, c_j, c_a, c_b = shares.shape
        tiles = jnp.transpose(shares.reshape(c_i, c_j, c_a, n_slab, c_b // n_slab), (3, 0, 1, 4, 2))
        tiles = tiles.reshape(n_slab, c_i * c_j, c_a * c_a)
        if ch == 0:
            outgoing = jnp.zeros((n_slab, i_rows * c_j, c_a * c_a), shares.dtype)
        outgoing = lax.dynamic_update_slice_in_dim(outgoing, tiles, ch * c_i * c_j, axis=1)
    shares = jnp.concatenate(share_parts, axis=0)

    i_n, j_n, a_n, b_n = shares.shape
    gathered = jnp.zeros((n_slab, j_n * i_n, a_n * a_n), shares.dtype)
    for d in range(n_slab):
        flat = lax.dynamic_slice_in_dim(outgoing, slab_at ^ d, 1, axis=0)
        pairs = [
            ((r * n_col + c) * n_slab + t, (c * n_col + r) * n_slab + (t ^ d))
            for r in range(n_row)
            for c in range(n_col)
            for t in range(n_slab)
        ]
        flat = lax.ppermute(flat, ("row", "col", "slab"), pairs)
        gathered = lax.dynamic_update_slice_in_dim(gathered, flat, slab_at ^ d, axis=0)
    gathered = gathered.reshape(n_slab, i_n, j_n, a_n, a_n)
    mirrored = jnp.transpose(gathered, (2, 1, 3, 0, 4)).reshape(shares.shape)
    return (shares + mirrored).astype(jnp.bfloat16)


def solution(mesh):
    return jax.shard_map(
        body,
        mesh=mesh,
        in_specs=(P("row", "col", "slab", None), P("row", "slab", "col", None), P(), P()),
        out_specs=P("row", "col", "slab", None),
        check_vma=False,
    )
```

```python
import jax
import jax.numpy as jnp
from jax import lax
from jax.sharding import PartitionSpec as P

OBLK = 12
VTILE = 32


def shifted(value, axis, fn):
    size = lax.axis_size(axis)
    return lax.ppermute(value, axis, [(src, fn(src) % size) for src in range(size)])


def int_mask(irreps, blocks, row_at, col_at, slab_at, c_cols, win_cols):
    c_ids = slab_at * c_cols + jnp.arange(c_cols, dtype=jnp.int32)
    b_ids = jnp.arange(win_cols, dtype=jnp.int32)
    label_c = jnp.take(irreps, blocks + c_ids // VTILE)
    label_b = jnp.take(irreps, blocks + b_ids // VTILE)
    occ = irreps[row_at] + irreps[col_at]
    parity = occ + label_c[:, None] + label_b[None, :]
    return parity % 2 == 0


def gather_row(ints, row_at):
    zpart = shifted(ints, "row", lambda r: r ^ 2)
    blocks = [ints, shifted(ints, "row", lambda r: r ^ 1), zpart, shifted(zpart, "row", lambda r: r ^ 1)]
    k_rows = ints.shape[0]
    whole = jnp.zeros((len(blocks) * k_rows,) + ints.shape[1:], ints.dtype)
    for u, blk in enumerate(blocks):
        whole = lax.dynamic_update_slice_in_dim(whole, blk, (row_at ^ u) * k_rows, axis=0)
    return whole


def ring_reduce_y(part, slab_at, split_axis):
    ny = lax.axis_size("slab") // 2
    width = part.shape[2] // ny
    y_at = slab_at // 2
    half = part.shape[split_axis] // 2
    halves = tuple(lax.slice_in_dim(part, h * half, (h + 1) * half, axis=split_axis) for h in range(2))
    dirs = (1, -1)
    acc = [None, None]
    for step in range(ny - 1):
        for h in range(2):
            d = dirs[h]
            chunk = (y_at - d * (step + 1)) % ny
            own = lax.dynamic_slice_in_dim(halves[h], chunk * width, width, axis=2)
            send = own if acc[h] is None else acc[h] + own
            acc[h] = shifted(send, "slab", lambda s, d=d: s + 2 * d)
    result = []
    for h in range(2):
        own = lax.dynamic_slice_in_dim(halves[h], y_at * width, width, axis=2)
        result.append(acc[h] + own)
    return jnp.concatenate(result, axis=split_axis)


def body(amplitudes, integrals, irreps, pair_mask):
    i_rows, k_rows, c_cols, win_cols = amplitudes.shape
    blocks = pair_mask.shape[0]
    row_at = lax.axis_index("row")
    col_at = lax.axis_index("col")
    slab_at = lax.axis_index("slab")
    n_slab = lax.axis_size("slab")

    mask = int_mask(irreps, blocks, row_at, col_at, slab_at, c_cols, win_cols)
    ints = jnp.where(mask[None, :, None, :], integrals, jnp.zeros_like(integrals))

    amp_all = lax.all_gather(amplitudes, "col", axis=1, tiled=True)
    keep = pair_mask[row_at, jnp.arange(amp_all.shape[1], dtype=jnp.int32) // OBLK] != 0
    int_abs = gather_row(ints, row_at)
    n_row = lax.axis_size("row")
    n_col = lax.axis_size("col")
    n_chunks = 3
    rows = i_rows // n_chunks
    share_parts = []
    for ch in range(n_chunks):
        amp_part = lax.slice_in_dim(amp_all, ch * rows, (ch + 1) * rows, axis=0)
        amp_part = jnp.where(keep[None, :, None, None], amp_part, jnp.zeros_like(amp_part))
        part = jnp.einsum("ikca,kcjb->ijab", amp_part, int_abs, preferred_element_type=jnp.float32)
        reduced_y = ring_reduce_y(part, slab_at, 1)
        zh = slab_at % 2
        width = reduced_y.shape[2] // 2
        mine = lax.dynamic_slice_in_dim(reduced_y, zh * width, width, axis=2)
        theirs = lax.dynamic_slice_in_dim(reduced_y, (1 - zh) * width, width, axis=2)
        shares = mine + shifted(theirs, "slab", lambda s: s ^ 1)
        share_parts.append(shares)
        c_i, c_j, c_a, c_b = shares.shape
        tiles = jnp.transpose(shares.reshape(c_i, c_j, c_a, n_slab, c_b // n_slab), (3, 0, 1, 4, 2))
        tiles = tiles.reshape(n_slab, c_i * c_j, c_a * c_a)
        if ch == 0:
            outgoing = jnp.zeros((n_slab, i_rows * c_j, c_a * c_a), shares.dtype)
        outgoing = lax.dynamic_update_slice_in_dim(outgoing, tiles, ch * c_i * c_j, axis=1)
    shares = jnp.concatenate(share_parts, axis=0)

    i_n, j_n, a_n, b_n = shares.shape
    gathered = jnp.zeros((n_slab, j_n * i_n, a_n * a_n), shares.dtype)
    for d in range(n_slab):
        flat = lax.dynamic_slice_in_dim(outgoing, slab_at ^ d, 1, axis=0)
        pairs = [
            ((r * n_col + c) * n_slab + t, (c * n_col + r) * n_slab + (t ^ d))
            for r in range(n_row)
            for c in range(n_col)
            for t in range(n_slab)
        ]
        flat = lax.ppermute(flat, ("row", "col", "slab"), pairs)
        gathered = lax.dynamic_update_slice_in_dim(gathered, flat, slab_at ^ d, axis=0)
    gathered = gathered.reshape(n_slab, i_n, j_n, a_n, a_n)
    mirrored = jnp.transpose(gathered, (2, 1, 3, 0, 4)).reshape(shares.shape)
    return (shares + mirrored).astype(jnp.bfloat16)


def solution(mesh):
    return jax.shard_map(
        body,
        mesh=mesh,
        in_specs=(P("row", "col", "slab", None), P("row", "slab", "col", None), P(), P()),
        out_specs=P("row", "col", "slab", None),
        check_vma=False,
    )
```

```python
import jax
import jax.numpy as jnp
from jax import lax
from jax.sharding import PartitionSpec as P

OBLK = 12
VTILE = 32


def shifted(value, axis, fn):
    size = lax.axis_size(axis)
    return lax.ppermute(value, axis, [(src, fn(src) % size) for src in range(size)])


def int_mask(irreps, blocks, row_at, col_at, slab_at, c_cols, win_cols):
    c_ids = slab_at * c_cols + jnp.arange(c_cols, dtype=jnp.int32)
    b_ids = jnp.arange(win_cols, dtype=jnp.int32)
    label_c = jnp.take(irreps, blocks + c_ids // VTILE)
    label_b = jnp.take(irreps, blocks + b_ids // VTILE)
    occ = irreps[row_at] + irreps[col_at]
    parity = occ + label_c[:, None] + label_b[None, :]
    return parity % 2 == 0


def gather_row(ints, row_at):
    zpart = shifted(ints, "row", lambda r: r ^ 2)
    blocks = [ints, shifted(ints, "row", lambda r: r ^ 1), zpart, shifted(zpart, "row", lambda r: r ^ 1)]
    k_rows = ints.shape[0]
    whole = jnp.zeros((len(blocks) * k_rows,) + ints.shape[1:], ints.dtype)
    for u, blk in enumerate(blocks):
        whole = lax.dynamic_update_slice_in_dim(whole, blk, (row_at ^ u) * k_rows, axis=0)
    return whole


def ring_reduce_y(part, slab_at, split_axis):
    ny = lax.axis_size("slab") // 2
    width = part.shape[2] // ny
    y_at = slab_at // 2
    half = part.shape[split_axis] // 2
    halves = tuple(lax.slice_in_dim(part, h * half, (h + 1) * half, axis=split_axis) for h in range(2))
    dirs = (1, -1)
    acc = [None, None]
    for step in range(ny - 1):
        for h in range(2):
            d = dirs[h]
            chunk = (y_at - d * (step + 1)) % ny
            own = lax.dynamic_slice_in_dim(halves[h], chunk * width, width, axis=2)
            send = own if acc[h] is None else acc[h] + own
            acc[h] = shifted(send, "slab", lambda s, d=d: s + 2 * d)
    result = []
    for h in range(2):
        own = lax.dynamic_slice_in_dim(halves[h], y_at * width, width, axis=2)
        result.append(acc[h] + own)
    return jnp.concatenate(result, axis=split_axis)


def body(amplitudes, integrals, irreps, pair_mask):
    i_rows, k_rows, c_cols, win_cols = amplitudes.shape
    blocks = pair_mask.shape[0]
    row_at = lax.axis_index("row")
    col_at = lax.axis_index("col")
    slab_at = lax.axis_index("slab")
    n_slab = lax.axis_size("slab")

    mask = int_mask(irreps, blocks, row_at, col_at, slab_at, c_cols, win_cols)
    ints = jnp.where(mask[None, :, None, :], integrals, jnp.zeros_like(integrals))

    amp_all = lax.all_gather(amplitudes, "col", axis=1, tiled=True)
    keep = pair_mask[row_at, jnp.arange(amp_all.shape[1], dtype=jnp.int32) // OBLK] != 0
    int_abs = gather_row(ints, row_at)
    n_row = lax.axis_size("row")
    n_col = lax.axis_size("col")
    n_chunks = 2
    rows = i_rows // n_chunks
    share_parts = []
    for ch in range(n_chunks):
        amp_part = lax.slice_in_dim(amp_all, ch * rows, (ch + 1) * rows, axis=0)
        amp_part = jnp.where(keep[None, :, None, None], amp_part, jnp.zeros_like(amp_part))
        part = jnp.einsum("ikca,kcjb->ijab", amp_part, int_abs, preferred_element_type=jnp.float32)
        reduced_y = ring_reduce_y(part, slab_at, 1)
        zh = slab_at % 2
        width = reduced_y.shape[2] // 2
        mine = lax.dynamic_slice_in_dim(reduced_y, zh * width, width, axis=2)
        theirs = lax.dynamic_slice_in_dim(reduced_y, (1 - zh) * width, width, axis=2)
        shares = mine + shifted(theirs, "slab", lambda s: s ^ 1)
        share_parts.append(shares)
        c_i, c_j, c_a, c_b = shares.shape
        tiles = jnp.transpose(shares.reshape(c_i, c_j, c_a, n_slab, c_b // n_slab), (3, 0, 1, 4, 2))
        tiles = tiles.reshape(n_slab, c_i * c_j, c_a * c_a)
        if ch == 0:
            outgoing = jnp.zeros((n_slab, i_rows * c_j, c_a * c_a), shares.dtype)
        outgoing = lax.dynamic_update_slice_in_dim(outgoing, tiles, ch * c_i * c_j, axis=1)
    shares = jnp.concatenate(share_parts, axis=0)

    i_n, j_n, a_n, b_n = shares.shape
    gathered = jnp.zeros((n_slab, j_n * i_n, a_n * a_n), shares.dtype)
    for d in range(n_slab):
        flat = lax.dynamic_slice_in_dim(outgoing, slab_at ^ d, 1, axis=0)
        pairs = [
            ((r * n_col + c) * n_slab + t, (c * n_col + r) * n_slab + (t ^ d))
            for r in range(n_row)
            for c in range(n_col)
            for t in range(n_slab)
        ]
        flat = lax.ppermute(flat, ("row", "col", "slab"), pairs)
        gathered = lax.dynamic_update_slice_in_dim(gathered, flat, slab_at ^ d, axis=0)
    gathered = gathered.reshape(n_slab, i_n, j_n, a_n, a_n)
    mirrored = jnp.transpose(gathered, (2, 1, 3, 0, 4)).reshape(shares.shape)
    return (shares + mirrored).astype(jnp.bfloat16)


def solution(mesh):
    return jax.shard_map(
        body,
        mesh=mesh,
        in_specs=(P("row", "col", "slab", None), P("row", "slab", "col", None), P(), P()),
        out_specs=P("row", "col", "slab", None),
        check_vma=False,
    )
```

```python
import jax
import jax.numpy as jnp
from jax import lax
from jax.sharding import PartitionSpec as P

OBLK = 12
VTILE = 32


def shifted(value, axis, fn):
    size = lax.axis_size(axis)
    return lax.ppermute(value, axis, [(src, fn(src) % size) for src in range(size)])


def int_mask(irreps, blocks, row_at, col_at, slab_at, c_cols, win_cols):
    c_ids = slab_at * c_cols + jnp.arange(c_cols, dtype=jnp.int32)
    b_ids = jnp.arange(win_cols, dtype=jnp.int32)
    label_c = jnp.take(irreps, blocks + c_ids // VTILE)
    label_b = jnp.take(irreps, blocks + b_ids // VTILE)
    occ = irreps[row_at] + irreps[col_at]
    parity = occ + label_c[:, None] + label_b[None, :]
    return parity % 2 == 0


def gather_row(ints, row_at):
    zpart = shifted(ints, "row", lambda r: r ^ 2)
    blocks = [ints, shifted(ints, "row", lambda r: r ^ 1), zpart, shifted(zpart, "row", lambda r: r ^ 1)]
    k_rows = ints.shape[0]
    whole = jnp.zeros((len(blocks) * k_rows,) + ints.shape[1:], ints.dtype)
    for u, blk in enumerate(blocks):
        whole = lax.dynamic_update_slice_in_dim(whole, blk, (row_at ^ u) * k_rows, axis=0)
    return whole


def ring_reduce_y(part, slab_at, split_axis):
    ny = lax.axis_size("slab") // 2
    width = part.shape[2] // ny
    y_at = slab_at // 2
    half = part.shape[split_axis] // 2
    halves = tuple(lax.slice_in_dim(part, h * half, (h + 1) * half, axis=split_axis) for h in range(2))
    dirs = (1, -1)
    acc = [None, None]
    for step in range(ny - 1):
        for h in range(2):
            d = dirs[h]
            chunk = (y_at - d * (step + 1)) % ny
            own = lax.dynamic_slice_in_dim(halves[h], chunk * width, width, axis=2)
            send = own if acc[h] is None else acc[h] + own
            acc[h] = shifted(send, "slab", lambda s, d=d: s + 2 * d)
    result = []
    for h in range(2):
        own = lax.dynamic_slice_in_dim(halves[h], y_at * width, width, axis=2)
        result.append(acc[h] + own)
    return jnp.concatenate(result, axis=split_axis)


def body(amplitudes, integrals, irreps, pair_mask):
    i_rows, k_rows, c_cols, win_cols = amplitudes.shape
    blocks = pair_mask.shape[0]
    row_at = lax.axis_index("row")
    col_at = lax.axis_index("col")
    slab_at = lax.axis_index("slab")
    n_slab = lax.axis_size("slab")

    mask = int_mask(irreps, blocks, row_at, col_at, slab_at, c_cols, win_cols)
    ints = jnp.where(mask[None, :, None, :], integrals, jnp.zeros_like(integrals))

    amp_all = lax.all_gather(amplitudes, "col", axis=1, tiled=True)
    keep = pair_mask[row_at, jnp.arange(amp_all.shape[1], dtype=jnp.int32) // OBLK] != 0
    int_abs = gather_row(ints, row_at)
    n_row = lax.axis_size("row")
    n_col = lax.axis_size("col")
    n_chunks = 3
    rows = i_rows // n_chunks
    share_parts = []
    for ch in range(n_chunks):
        amp_part = lax.slice_in_dim(amp_all, ch * rows, (ch + 1) * rows, axis=0)
        amp_part = jnp.where(keep[None, :, None, None], amp_part, jnp.zeros_like(amp_part))
        part = jnp.einsum("ikca,kcjb->ijab", amp_part, int_abs, preferred_element_type=jnp.float32)
        reduced_y = ring_reduce_y(part, slab_at, 0)
        zh = slab_at % 2
        width = reduced_y.shape[2] // 2
        mine = lax.dynamic_slice_in_dim(reduced_y, zh * width, width, axis=2)
        theirs = lax.dynamic_slice_in_dim(reduced_y, (1 - zh) * width, width, axis=2)
        shares = mine + shifted(theirs, "slab", lambda s: s ^ 1)
        share_parts.append(shares)
        c_i, c_j, c_a, c_b = shares.shape
        tiles = jnp.transpose(shares.reshape(c_i, c_j, c_a, n_slab, c_b // n_slab), (3, 0, 1, 4, 2))
        tiles = tiles.reshape(n_slab, c_i * c_j, c_a * c_a)
        if ch == 0:
            outgoing = jnp.zeros((n_slab, i_rows * c_j, c_a * c_a), shares.dtype)
        outgoing = lax.dynamic_update_slice_in_dim(outgoing, tiles, ch * c_i * c_j, axis=1)
    shares = jnp.concatenate(share_parts, axis=0)

    i_n, j_n, a_n, b_n = shares.shape
    gathered = jnp.zeros((n_slab, j_n * i_n, a_n * a_n), shares.dtype)
    for d in range(n_slab):
        flat = lax.dynamic_slice_in_dim(outgoing, slab_at ^ d, 1, axis=0)
        pairs = [
            ((r * n_col + c) * n_slab + t, (c * n_col + r) * n_slab + (t ^ d))
            for r in range(n_row)
            for c in range(n_col)
            for t in range(n_slab)
        ]
        flat = lax.ppermute(flat, ("row", "col", "slab"), pairs)
        gathered = lax.dynamic_update_slice_in_dim(gathered, flat, slab_at ^ d, axis=0)
    gathered = gathered.reshape(n_slab, i_n, j_n, a_n, a_n)
    mirrored = jnp.transpose(gathered, (2, 1, 3, 0, 4)).reshape(shares.shape)
    return (shares + mirrored).astype(jnp.bfloat16)


def solution(mesh):
    return jax.shard_map(
        body,
        mesh=mesh,
        in_specs=(P("row", "col", "slab", None), P("row", "slab", "col", None), P(), P()),
        out_specs=P("row", "col", "slab", None),
        check_vma=False,
    )
```
